512 devices in a mesh: row: 64 (over x, z), col: 8 (over y, core).
Axes of the slice: x: 4, y: 4, z: 16, core: 2. Of those that a mesh axis runs over, the one named last changes fastest.
Arguments:
- current: bfloat16 [2, 256, 32, 4, 128], P(None, 'row', 'col'), may hold values from -6 to 6
- probe: bfloat16 [2, 256, 32, 4, 128], P(None, 'row', 'col'), may hold values from -6 to 6
- near_list: int32 [256, 32, 2], P('row', 'col'), may hold values from 0 to 9, as said below
- near_blocks: bfloat16 [2, 256, 32, 2, 128, 128], P(None, 'row', 'col'), may hold values from -0.25 to 0.25
- radiation: bfloat16 [2, 128, 128], replicated, may hold values from -0.375 to 0.375
- reception: bfloat16 [2, 128, 128], replicated, may hold values from -0.375 to 0.375
- interp: float32 [256, 128], replicated, may hold values from -0.5 to 0.5
- phase: float32 [16, 256], replicated, may hold values from -3.140625 to 3.140625
- leaf_table: float32 [2, 15, 15, 128], replicated, may hold values from -0.36 to 0.36
- coarse_table: bfloat16 [2, 127, 15, 256], replicated, may hold values from -0.023925781 to 0.023925781
Outputs:
- forward_out: float32 [2, 256, 32, 4, 128], P(None, 'row', 'col')
- adjoint_out: float32 [2, 256, 32, 4, 128], P(None, 'row', 'col')
The draws below stay inside these ranges and needn't reach their ends.
Inputs may be any that keep to these rules, and one draw needn't show every extreme that they name: `near_list`: the 2 slots of a box hold distinct codes; only slots after the first may be empty (code 9).
All inputs are finite; a program needn't handle non-finite values.
Results may differ from the reference program's by a relative error of at most 0.0027.
Values may be sent and summed in bfloat16 or wider, within the bound.
No kernel may reach another device: no remote copies, remote signals or barrier semaphores. Data moves between devices by JAX's collectives and lax.ppermute only.
A program may use at most 128 MiB of HBM per device.

```python
import jax
import jax.numpy as jnp
from jax import lax

P_SIZE = 128
Q0 = 128
Q1 = 256
K = 2
SIDE = 4
RHS = 4
NR = 256
NC = 32
OFFS = 15
TROWS = 127
TCOLS = 15
N_ROW = 64
N_COL = 8


def draw_near_list(key, part):
    key_order = jax.random.fold_in(key, 11)
    key_empty = jax.random.fold_in(key, 12)
    scores = jax.random.randint(key_order, (NR, NC, 9), 0, 2 ** 20) * 16 + jnp.arange(9, dtype=jnp.int32)
    ranked = jnp.argsort(scores, axis=-1, stable=True)[..., :K].astype(jnp.int32)
    empty_slot = jax.random.randint(key_empty, (NR, NC, K), 0, 4) == 0
    slot_index = jnp.arange(K, dtype=jnp.int32)
    empty_slot = empty_slot & (slot_index > 0)
    return jnp.where(empty_slot, 9, ranked).astype(jnp.int32)


def level_of(rng, extent, split, least, top_value):
    gain = 1.0
    for axis_at, blocks in split:
        heights = jax.random.uniform(jax.random.fold_in(jax.random.fold_in(rng, 6), axis_at), (blocks,), jnp.float32, least / len(split), top_value / len(split))
        gain = gain * jnp.repeat(jnp.exp(heights), extent[axis_at] // blocks).reshape((-1,) + (1,) * (len(extent) - 1 - axis_at))
    return gain


def bell_draw(stream_key, extent, scale, limit, shards=(), kind=jnp.bfloat16):
    result = jax.random.normal(stream_key, extent, jnp.float32) * scale
    if len(shards) > 0:
        result = level_of(stream_key, extent, shards, -0.22, 0.18) * result
    return jnp.clip(result, min=-limit, max=limit).astype(kind)


def setup_inputs(seed: int = 0) -> dict:
    streams_of = jax.random.split(jax.random.key(seed), 11)
    current = bell_draw(streams_of[0], (2, NR, NC, RHS, P_SIZE), 1.0, 6.0, ((1, 64), (2, 8)))
    probe = bell_draw(streams_of[1], (2, NR, NC, RHS, P_SIZE), 1.0, 6.0, ((1, 64), (2, 8)))
    near_list = draw_near_list(jax.random.fold_in(streams_of[10], 71), 0)
    near_blocks = bell_draw(streams_of[3], (2, NR, NC, K, P_SIZE, P_SIZE), (2 * K * P_SIZE) ** -0.5, 0.25, ((1, 64), (2, 8)))
    radiation = bell_draw(streams_of[4], (2, Q0, P_SIZE), (2 * P_SIZE) ** -0.5, 0.375)
    reception = bell_draw(streams_of[5], (2, P_SIZE, Q0), (2 * Q0) ** -0.5, 0.375)
    interp = bell_draw(streams_of[6], (Q1, Q0), Q0 ** -0.5, 0.5, (), jnp.float32)
    phase = jnp.clip(jax.random.uniform(streams_of[7], (SIDE * SIDE, Q1), jnp.float32, -3.140625, 3.140625), -3.140625, 3.140625)
    leaf_table = bell_draw(streams_of[8], (2, OFFS, OFFS, Q0), 0.06, 0.36, (), jnp.float32)
    coarse_table = bell_draw(streams_of[9], (2, TROWS, TCOLS, Q1), 0.004, 0.023925781)
    return dict(current=current, probe=probe, near_list=near_list, near_blocks=near_blocks, radiation=radiation, reception=reception, interp=interp, phase=phase, leaf_table=leaf_table, coarse_table=coarse_table)


HIGH = lax.Precision.HIGHEST


def complex_mul(left_re, left_im, right_re, right_im):
    return left_re * right_re - left_im * right_im, left_re * right_im + left_im * right_re


def conj_flip(table, axes):
    flipped = jnp.flip(table, axes)
    return jnp.stack([flipped[0], -flipped[1]])


def near_part(current, probe, near_list, near_blocks):
    pad_cur = jnp.pad(current.astype(jnp.float32), ((0, 0), (1, 1), (1, 1), (0, 0), (0, 0)))

    def one_row(row_index):
        row_index = row_index.astype(jnp.int32)
        blocks = lax.dynamic_index_in_dim(near_blocks, row_index, 1, keepdims=False).astype(jnp.float32)
        slot_codes = lax.dynamic_index_in_dim(near_list, row_index, 0, keepdims=False)
        band = lax.dynamic_slice_in_dim(pad_cur, row_index, 3, 1)
        shifted = jnp.stack([band[:, offset_code // 3, offset_code % 3:offset_code % 3 + NC] for offset_code in range(9)])
        one_hot = (slot_codes[..., None] == jnp.arange(9, dtype=jnp.int32)).astype(jnp.float32)
        picked = jnp.einsum('cko,oxcmp->xkcmp', one_hot, shifted, precision=HIGH)
        blocks_re, blocks_im = blocks[0], blocks[1]
        fwd_re = jnp.einsum('ckpq,kcmq->cmp', blocks_re, picked[0], precision=HIGH) - jnp.einsum('ckpq,kcmq->cmp', blocks_im, picked[1], precision=HIGH)
        fwd_im = jnp.einsum('ckpq,kcmq->cmp', blocks_re, picked[1], precision=HIGH) + jnp.einsum('ckpq,kcmq->cmp', blocks_im, picked[0], precision=HIGH)
        probe_row = lax.dynamic_index_in_dim(probe, row_index, 1, keepdims=False).astype(jnp.float32)
        back_re = jnp.einsum('ckpq,cmp->kcmq', blocks_re, probe_row[0], precision=HIGH) + jnp.einsum('ckpq,cmp->kcmq', blocks_im, probe_row[1], precision=HIGH)
        back_im = jnp.einsum('ckpq,cmp->kcmq', blocks_re, probe_row[1], precision=HIGH) - jnp.einsum('ckpq,cmp->kcmq', blocks_im, probe_row[0], precision=HIGH)
        return jnp.stack([fwd_re, fwd_im]), jnp.stack([back_re, back_im])

    fwd_rows, contrib = lax.map(one_row, jnp.arange(NR, dtype=jnp.int32))
    near_fwd = jnp.moveaxis(fwd_rows, 0, 1)
    contrib = jnp.moveaxis(contrib, 0, 2)
    placed = jnp.zeros((2, NR + 2, NC + 2, RHS, P_SIZE), jnp.float32)
    for offset_code in range(9):
        mask_code = (near_list == offset_code).astype(jnp.float32)
        selected = jnp.einsum('rck,xkrcmp->xrcmp', mask_code, contrib, precision=HIGH)
        placed = placed.at[:, offset_code // 3:offset_code // 3 + NR, offset_code % 3:offset_code % 3 + NC].add(selected)
    near_adj = placed[:, 1:NR + 1, 1:NC + 1]
    return near_fwd, near_adj


def far_part(vector, rad_re, rad_im, rcv_re, rcv_im, leaf_table, coarse_table, interp, phase):
    values = vector.astype(jnp.float32)
    rad_re = rad_re.astype(jnp.float32)
    rad_im = rad_im.astype(jnp.float32)
    out_re = jnp.einsum('rcmp,qp->rcmq', values[0], rad_re, precision=HIGH) - jnp.einsum('rcmp,qp->rcmq', values[1], rad_im, precision=HIGH)
    out_im = jnp.einsum('rcmp,qp->rcmq', values[0], rad_im, precision=HIGH) + jnp.einsum('rcmp,qp->rcmq', values[1], rad_re, precision=HIGH)
    reach = 2 * SIDE - 1
    pad_re = jnp.pad(out_re, ((reach, reach), (reach, reach), (0, 0), (0, 0)))
    pad_im = jnp.pad(out_im, ((reach, reach), (reach, reach), (0, 0), (0, 0)))
    row_ids = jnp.arange(NR, dtype=jnp.int32)
    col_ids = jnp.arange(NC, dtype=jnp.int32)

    def leaf_step(index, carry):
        acc_re, acc_im = carry
        index = index.astype(jnp.int32)
        row_off = index // OFFS - reach
        col_off = index % OFFS - reach
        start_row = (reach + row_off).astype(jnp.int32)
        start_col = (reach + col_off).astype(jnp.int32)
        zero = jnp.zeros((), jnp.int32)
        src_re = lax.dynamic_slice(pad_re, (start_row, start_col, zero, zero), (NR, NC, RHS, Q0))
        src_im = lax.dynamic_slice(pad_im, (start_row, start_col, zero, zero), (NR, NC, RHS, Q0))
        ok_rows = jnp.abs((row_ids + row_off) // SIDE - row_ids // SIDE) <= 1
        ok_cols = jnp.abs((col_ids + col_off) // SIDE - col_ids // SIDE) <= 1
        adjacent = (jnp.abs(row_off) <= 1) & (jnp.abs(col_off) <= 1)
        valid = (ok_rows[:, None] & ok_cols[None, :] & jnp.logical_not(adjacent)).astype(jnp.float32)
        coeff = lax.dynamic_slice(leaf_table, (zero, (index // OFFS).astype(jnp.int32), (index % OFFS).astype(jnp.int32), zero), (2, 1, 1, Q0)).reshape(2, Q0)
        part_re, part_im = complex_mul(coeff[0], coeff[1], src_re, src_im)
        return acc_re + part_re * valid[:, :, None, None], acc_im + part_im * valid[:, :, None, None]

    zeros_leaf = jnp.zeros((NR, NC, RHS, Q0), jnp.float32)
    leaf_re, leaf_im = lax.fori_loop(0, OFFS * OFFS, leaf_step, (zeros_leaf, zeros_leaf))

    interp_re = jnp.einsum('kq,rcmq->rcmk', interp, out_re, precision=HIGH).reshape(N_ROW, SIDE, N_COL, SIDE, RHS, Q1)
    interp_im = jnp.einsum('kq,rcmq->rcmk', interp, out_im, precision=HIGH).reshape(N_ROW, SIDE, N_COL, SIDE, RHS, Q1)
    angles = phase.reshape(SIDE, SIDE, Q1)
    cos_ph = jnp.cos(angles)[None, :, None, :, None, :]
    sin_ph = jnp.sin(angles)[None, :, None, :, None, :]
    top_re = jnp.sum(cos_ph * interp_re - sin_ph * interp_im, axis=(1, 3))
    top_im = jnp.sum(cos_ph * interp_im + sin_ph * interp_re, axis=(1, 3))
    top_b = jnp.stack([top_re, top_im]).astype(jnp.bfloat16)
    top_f = lax.optimization_barrier(top_b).astype(jnp.float32)

    table_f = coarse_table.astype(jnp.float32)
    col_index = jnp.arange(N_COL, dtype=jnp.int32)
    col_diff = col_index[:, None] - col_index[None, :]
    row_index_all = jnp.arange(N_ROW, dtype=jnp.int32)

    def one_target(target_row):
        target_row = target_row.astype(jnp.int32)
        row_pick = jnp.take(table_f, target_row - row_index_all + N_ROW - 1, axis=1)
        joint = row_pick[:, :, col_diff + N_COL - 1]
        distant = (jnp.abs(target_row - row_index_all)[:, None, None] > 1) | (jnp.abs(col_diff)[None] > 1)
        weight = distant.astype(jnp.float32)[..., None]
        joint_re = joint[0] * weight
        joint_im = joint[1] * weight
        got_re = jnp.einsum('scdq,sdmq->cmq', joint_re, top_f[0], precision=HIGH) - jnp.einsum('scdq,sdmq->cmq', joint_im, top_f[1], precision=HIGH)
        got_im = jnp.einsum('scdq,sdmq->cmq', joint_re, top_f[1], precision=HIGH) + jnp.einsum('scdq,sdmq->cmq', joint_im, top_f[0], precision=HIGH)
        return jnp.stack([got_re, got_im])

    coarse_in = jnp.moveaxis(lax.map(one_target, row_index_all), 0, 1)
    in_re = coarse_in[0][:, None, :, None]
    in_im = coarse_in[1][:, None, :, None]
    back_re = (cos_ph * in_re + sin_ph * in_im).reshape(NR, NC, RHS, Q1)
    back_im = (cos_ph * in_im - sin_ph * in_re).reshape(NR, NC, RHS, Q1)
    spread_re = jnp.einsum('kq,rcmk->rcmq', interp, back_re, precision=HIGH)
    spread_im = jnp.einsum('kq,rcmk->rcmq', interp, back_im, precision=HIGH)
    incoming = jnp.stack([leaf_re + spread_re, leaf_im + spread_im]).astype(jnp.bfloat16)
    incoming = lax.optimization_barrier(incoming).astype(jnp.float32)
    rcv_re = rcv_re.astype(jnp.float32)
    rcv_im = rcv_im.astype(jnp.float32)
    res_re = jnp.einsum('rcmq,pq->rcmp', incoming[0], rcv_re, precision=HIGH) - jnp.einsum('rcmq,pq->rcmp', incoming[1], rcv_im, precision=HIGH)
    res_im = jnp.einsum('rcmq,pq->rcmp', incoming[0], rcv_im, precision=HIGH) + jnp.einsum('rcmq,pq->rcmp', incoming[1], rcv_re, precision=HIGH)
    return jnp.stack([res_re, res_im])


def reference(current, probe, near_list, near_blocks, radiation, reception, interp, phase, leaf_table, coarse_table):
    near_fwd, near_adj = near_part(current, probe, near_list, near_blocks)
    far_fwd = far_part(current, radiation[0], radiation[1], reception[0], reception[1], leaf_table, coarse_table, interp, phase)
    far_adj = far_part(probe, reception[0].T, -reception[1].T, radiation[0].T, -radiation[1].T, conj_flip(leaf_table, (1, 2)), conj_flip(coarse_table, (1, 2)), interp, phase)
    return near_fwd + far_fwd, near_adj + far_adj
```

```python
import jax
import jax.numpy as jnp
from jax import lax
from jax.sharding import PartitionSpec as P

HIGH = lax.Precision.HIGHEST


def with_halo(cells, sides, width):
    for axis, dim in sides:
        count = lax.axis_size(axis)
        ends = count - 1
        head = lax.slice_in_dim(cells, 0, width, axis=dim)
        tail = lax.slice_in_dim(cells, cells.shape[dim] - width, cells.shape[dim], axis=dim)
        cells = jnp.concatenate(
            [
                lax.ppermute(tail, axis, [(i, (i + 1) % count) for i in range(ends)]),
                cells,
                lax.ppermute(head, axis, [((i + 1) % count, i) for i in range(ends)]),
            ],
            axis=dim,
        )
    return cells


def from_behind(block, axis, distance):
    devices = range(lax.axis_size(axis))
    route = [(i - distance, i) for i in devices if i - distance in devices]
    return lax.ppermute(block, axis, route)


def complex_mul(left_re, left_im, right_re, right_im):
    return (left_re * right_re - left_im * right_im, left_re * right_im + left_im * right_re)


def conj_flip(table, axes):
    flipped = jnp.flip(table, axes)
    return jnp.stack([flipped[0], -flipped[1]])


def product(form, left, right):
    return jnp.einsum(form, left, right, preferred_element_type=jnp.float32)


def near_field(current, probe, near_list, near_blocks):
    box_side = current.shape[1]
    one_hot = (near_list[..., None] == jnp.arange(9)).astype(jnp.bfloat16)
    blocks_re = near_blocks[0]
    blocks_im = near_blocks[1]
    padded = with_halo(current, (("row", 1), ("col", 2)), 1)
    shifted = jnp.stack(
        [
            padded[
                :,
                offset_code // 3 : offset_code // 3 + box_side,
                offset_code % 3 : offset_code % 3 + box_side,
            ]
            for offset_code in range(9)
        ]
    )
    picked = product("rcko,oxrcmp->xkrcmp", one_hot, shifted).astype(jnp.bfloat16)
    fwd_re = product("rckpq,krcmq->rcmp", blocks_re, picked[0]) - product(
        "rckpq,krcmq->rcmp", blocks_im, picked[1]
    )
    fwd_im = product("rckpq,krcmq->rcmp", blocks_re, picked[1]) + product(
        "rckpq,krcmq->rcmp", blocks_im, picked[0]
    )
    near_fwd = jnp.stack([fwd_re, fwd_im])
    back_re = product("rckpq,rcmp->krcmq", blocks_re, probe[0]) + product(
        "rckpq,rcmp->krcmq", blocks_im, probe[1]
    )
    back_im = product("rckpq,rcmp->krcmq", blocks_re, probe[1]) - product(
        "rckpq,rcmp->krcmq", blocks_im, probe[0]
    )
    contrib = jnp.stack([back_re, back_im])
    placed_all = jnp.einsum(
        "rcko,xkrcmp->oxrcmp", one_hot.astype(jnp.float32), contrib, precision=HIGH
    )
    placed = jnp.zeros((2, box_side + 2, box_side + 2) + contrib.shape[4:], jnp.float32)
    for offset_code in range(9):
        placed = placed.at[
            :,
            offset_code // 3 : offset_code // 3 + box_side,
            offset_code % 3 : offset_code % 3 + box_side,
        ].add(placed_all[offset_code])
    for step_dir, send_row, keep_row in ((1, box_side + 1, 1), (-1, 0, box_side)):
        arrived = from_behind(placed[:, send_row], "row", step_dir)
        placed = placed.at[:, keep_row].add(arrived)
    for step_dir, send_col, keep_col in ((1, box_side + 1, 1), (-1, 0, box_side)):
        arrived = from_behind(placed[:, 1 : box_side + 1, send_col], "col", step_dir)
        placed = placed.at[:, 1 : box_side + 1, keep_col].add(arrived)
    return (near_fwd, placed[:, 1 : box_side + 1, 1 : box_side + 1])


def far_field(vectors, rad_tab, rcv_tab, leaf_tab, coarse_tab, interp, phase):
    box_side = vectors.shape[2]
    span = 3 * box_side
    reach = 2 * box_side - 1
    out_re = product("srcmp,sqp->srcmq", vectors[:, 0], rad_tab[:, 0]) - product(
        "srcmp,sqp->srcmq", vectors[:, 1], rad_tab[:, 1]
    )
    out_im = product("srcmp,sqp->srcmq", vectors[:, 0], rad_tab[:, 1]) + product(
        "srcmp,sqp->srcmq", vectors[:, 1], rad_tab[:, 0]
    )
    leaf_out = jnp.stack([out_re, out_im], 1)
    window = with_halo(leaf_out, (("row", 2), ("col", 3)), box_side)
    offsets = jnp.arange(2 * reach + 1) - reach
    near_offset = jnp.abs(offsets) <= 1
    keep = 1.0 - (near_offset[:, None] & near_offset[None, :]).astype(jnp.float32)
    masked = leaf_tab * keep[None, None, :, :, None]
    rows_in = []
    for row_pos in range(box_side):
        cols_in = []
        for col_pos in range(box_side):
            row_first = box_side - 1 - row_pos
            col_first = box_side - 1 - col_pos
            coeffs = masked[:, :, row_first : row_first + span, col_first : col_first + span]
            part_re, part_im = complex_mul(
                coeffs[:, 0, :, :, None], coeffs[:, 1, :, :, None], window[:, 0], window[:, 1]
            )
            cols_in.append(jnp.stack([part_re.sum((1, 2)), part_im.sum((1, 2))], 1))
        rows_in.append(jnp.stack(cols_in, 2))
    leaf_in = jnp.stack(rows_in, 2)
    interpolated = jnp.einsum("kq,sxrcmq->sxrcmk", interp, leaf_out, precision=HIGH)
    angles = phase.reshape(box_side, box_side, -1)
    cos_ph = jnp.cos(angles)[:, :, None, :]
    sin_ph = jnp.sin(angles)[:, :, None, :]
    top_re = (cos_ph * interpolated[:, 0] - sin_ph * interpolated[:, 1]).sum((1, 2))
    top_im = (cos_ph * interpolated[:, 1] + sin_ph * interpolated[:, 0]).sum((1, 2))
    top_b = jnp.stack([top_re, top_im], 1).astype(jnp.bfloat16)
    row_idx = lax.axis_index("row")
    col_idx = lax.axis_index("col")
    row_count = lax.axis_size("row")
    col_count = lax.axis_size("col")
    flat_tab = coarse_tab.reshape(
        coarse_tab.shape[0], 2, coarse_tab.shape[2] * coarse_tab.shape[3], coarse_tab.shape[4]
    )
    portion = lax.all_gather(top_b[:, :, None], ("row", "col"), axis=2, tiled=True)
    sources = jnp.arange(portion.shape[2])
    src_rows = sources // col_count
    src_cols = sources % col_count
    flat_index = (row_idx - src_rows + row_count - 1) * (2 * col_count - 1) + (
        col_idx - src_cols + col_count - 1
    )
    coeff = jnp.take(flat_tab, flat_index, axis=2).astype(jnp.float32)
    distant = ((jnp.abs(row_idx - src_rows) > 1) | (jnp.abs(col_idx - src_cols) > 1)).astype(
        jnp.float32
    )
    coef_re = coeff[:, 0] * distant[None, :, None]
    coef_im = coeff[:, 1] * distant[None, :, None]
    values = portion.astype(jnp.float32)
    got_re = jnp.einsum("snq,snmq->smq", coef_re, values[:, 0], precision=HIGH) - jnp.einsum(
        "snq,snmq->smq", coef_im, values[:, 1], precision=HIGH
    )
    got_im = jnp.einsum("snq,snmq->smq", coef_re, values[:, 1], precision=HIGH) + jnp.einsum(
        "snq,snmq->smq", coef_im, values[:, 0], precision=HIGH
    )
    coarse_in = jnp.stack([got_re, got_im], 1)
    in_re = coarse_in[:, 0][:, None, None]
    in_im = coarse_in[:, 1][:, None, None]
    back_re = cos_ph * in_re + sin_ph * in_im
    back_im = cos_ph * in_im - sin_ph * in_re
    spread = jnp.einsum(
        "kq,sxrcmk->sxrcmq", interp, jnp.stack([back_re, back_im], 1), precision=HIGH
    )
    incoming = (leaf_in + spread).astype(jnp.bfloat16)
    res_re = product("srcmq,spq->srcmp", incoming[:, 0], rcv_tab[:, 0]) - product(
        "srcmq,spq->srcmp", incoming[:, 1], rcv_tab[:, 1]
    )
    res_im = product("srcmq,spq->srcmp", incoming[:, 0], rcv_tab[:, 1]) + product(
        "srcmq,spq->srcmp", incoming[:, 1], rcv_tab[:, 0]
    )
    return jnp.stack([res_re, res_im], 1)


def per_device(
    current,
    probe,
    near_list,
    near_blocks,
    radiation,
    reception,
    interp,
    phase,
    leaf_table,
    coarse_table,
):
    near_fwd, near_adj = near_field(current, probe, near_list, near_blocks)
    fwd_set = (radiation, reception, leaf_table, coarse_table)
    adj_set = (
        jnp.stack([reception[0].T, -reception[1].T]),
        jnp.stack([radiation[0].T, -radiation[1].T]),
        conj_flip(leaf_table, (1, 2)),
        conj_flip(coarse_table, (1, 2)),
    )
    far_both = far_field(
        jnp.stack([current, probe]),
        jnp.stack([fwd_set[0], adj_set[0]]),
        jnp.stack([fwd_set[1], adj_set[1]]),
        jnp.stack([fwd_set[2], adj_set[2]]),
        jnp.stack([fwd_set[3], adj_set[3]]),
        interp,
        phase,
    )
    far_fwd = far_both[0]
    far_adj = far_both[1]
    return (near_fwd + far_fwd, near_adj + far_adj)


def solution(mesh):
    placed = (
        P(None, "row", "col", None, None),
        P(None, "row", "col", None, None),
        P("row", "col", None),
        P(None, "row", "col", None, None, None),
        P(),
        P(),
        P(),
        P(),
        P(),
        P(),
    )
    return jax.shard_map(
        per_device,
        mesh=mesh,
        in_specs=placed,
        out_specs=(P(None, "row", "col", None, None), P(None, "row", "col", None, None)),
        check_vma=False,
    )
```

```python
import jax
import jax.numpy as jnp
from jax import lax
from jax.sharding import PartitionSpec as P

HIGH = lax.Precision.HIGHEST


def with_halo(cells, sides, width):
    for axis, dim in sides:
        count = lax.axis_size(axis)
        ends = count - 1
        head = lax.slice_in_dim(cells, 0, width, axis=dim)
        tail = lax.slice_in_dim(cells, cells.shape[dim] - width, cells.shape[dim], axis=dim)
        cells = jnp.concatenate(
            [
                lax.ppermute(tail, axis, [(i, (i + 1) % count) for i in range(ends)]),
                cells,
                lax.ppermute(head, axis, [((i + 1) % count, i) for i in range(ends)]),
            ],
            axis=dim,
        )
    return cells


def from_behind(block, axis, distance):
    devices = range(lax.axis_size(axis))
    route = [(i - distance, i) for i in devices if i - distance in devices]
    return lax.ppermute(block, axis, route)


def complex_mul(left_re, left_im, right_re, right_im):
    return (left_re * right_re - left_im * right_im, left_re * right_im + left_im * right_re)


def conj_flip(table, axes):
    flipped = jnp.flip(table, axes)
    return jnp.stack([flipped[0], -flipped[1]])


def product(form, left, right):
    return jnp.einsum(form, left, right, preferred_element_type=jnp.float32)


def near_field(current, probe, near_list, near_blocks):
    box_side = current.shape[1]
    one_hot = (near_list[..., None] == jnp.arange(9)).astype(jnp.bfloat16)
    blocks_re = near_blocks[0]
    blocks_im = near_blocks[1]
    padded = with_halo(current, (("row", 1), ("col", 2)), 1)
    shifted = jnp.stack(
        [
            padded[
                :,
                offset_code // 3 : offset_code // 3 + box_side,
                offset_code % 3 : offset_code % 3 + box_side,
            ]
            for offset_code in range(9)
        ]
    )
    picked = product("rcko,oxrcmp->xkrcmp", one_hot, shifted).astype(jnp.bfloat16)
    fwd_re = product("rckpq,krcmq->rcmp", blocks_re, picked[0]) - product(
        "rckpq,krcmq->rcmp", blocks_im, picked[1]
    )
    fwd_im = product("rckpq,krcmq->rcmp", blocks_re, picked[1]) + product(
        "rckpq,krcmq->rcmp", blocks_im, picked[0]
    )
    near_fwd = jnp.stack([fwd_re, fwd_im])
    back_re = product("rckpq,rcmp->krcmq", blocks_re, probe[0]) + product(
        "rckpq,rcmp->krcmq", blocks_im, probe[1]
    )
    back_im = product("rckpq,rcmp->krcmq", blocks_re, probe[1]) - product(
        "rckpq,rcmp->krcmq", blocks_im, probe[0]
    )
    contrib = jnp.stack([back_re, back_im])
    placed_all = jnp.einsum(
        "rcko,xkrcmp->oxrcmp", one_hot.astype(jnp.float32), contrib, precision=HIGH
    )
    placed = jnp.zeros((2, box_side + 2, box_side + 2) + contrib.shape[4:], jnp.float32)
    for offset_code in range(9):
        placed = placed.at[
            :,
            offset_code // 3 : offset_code // 3 + box_side,
            offset_code % 3 : offset_code % 3 + box_side,
        ].add(placed_all[offset_code])
    for step_dir, send_row, keep_row in ((1, box_side + 1, 1), (-1, 0, box_side)):
        arrived = from_behind(placed[:, send_row], "row", step_dir)
        placed = placed.at[:, keep_row].add(arrived)
    for step_dir, send_col, keep_col in ((1, box_side + 1, 1), (-1, 0, box_side)):
        arrived = from_behind(placed[:, 1 : box_side + 1, send_col], "col", step_dir)
        placed = placed.at[:, 1 : box_side + 1, keep_col].add(arrived)
    return (near_fwd, placed[:, 1 : box_side + 1, 1 : box_side + 1])


def gather_ordered(block, axis):
    count = lax.axis_size(axis)
    index = lax.axis_index(axis)
    held = block[None]
    step = 1
    while step < count:
        other = lax.ppermute(held, axis, [(i, i ^ step) for i in range(count)])
        lower = (index & step) == 0
        held = jnp.where(
            lower, jnp.concatenate([held, other], 0), jnp.concatenate([other, held], 0)
        )
        step *= 2
    return held


def scatter_sum(parts, axis):
    count = lax.axis_size(axis)
    index = lax.axis_index(axis)
    held = parts
    step = count // 2
    while step >= 1:
        half = held.shape[0] // 2
        upper = (index & step) != 0
        send = jnp.where(upper, held[:half], held[half:])
        keep = jnp.where(upper, held[half:], held[:half])
        held = keep + lax.ppermute(send, axis, [(i, i ^ step) for i in range(count)])
        step //= 2
    return held[0]


def coarse_exchange(top_b, coarse_tab):
    row_count = lax.axis_size("row")
    col_count = lax.axis_size("col")
    row_idx = lax.axis_index("row")
    col_idx = lax.axis_index("col")
    sources = gather_ordered(top_b, "row").astype(jnp.float32)
    zero = jnp.zeros((), jnp.int32)
    fwd_tab = coarse_tab[0]
    fwd = lax.dynamic_slice(
        fwd_tab,
        (zero, row_idx, col_count - 1 - col_idx, zero),
        (2, row_count, col_count, fwd_tab.shape[-1]),
    )
    fwd = jnp.flip(fwd, 1)
    adj = lax.dynamic_slice(
        fwd_tab,
        (zero, row_count - 1 - row_idx, col_idx, zero),
        (2, row_count, col_count, fwd_tab.shape[-1]),
    )
    adj = jnp.flip(adj, 2)
    adj = jnp.stack([adj[0], -adj[1]])
    coeff = jnp.stack([fwd, adj]).astype(jnp.float32)
    src_rows = jnp.arange(row_count)
    dst_cols = jnp.arange(col_count)
    distant = (jnp.abs(row_idx - src_rows)[:, None] > 1) | (jnp.abs(dst_cols - col_idx)[None, :] > 1)
    weight = distant.astype(jnp.float32)[None, :, :, None]
    coef_re = coeff[:, 0] * weight
    coef_im = coeff[:, 1] * weight
    val_re = jnp.moveaxis(sources[:, :, 0], 0, 1)[:, :, None]
    val_im = jnp.moveaxis(sources[:, :, 1], 0, 1)[:, :, None]
    c_re = coef_re[:, :, :, None]
    c_im = coef_im[:, :, :, None]
    got_re = (c_re * val_re - c_im * val_im).sum(1)
    got_im = (c_re * val_im + c_im * val_re).sum(1)
    parts = jnp.moveaxis(jnp.stack([got_re, got_im], 1), 2, 0)
    return scatter_sum(parts, "col")


def far_field(vectors, rad_tab, rcv_tab, leaf_tab, coarse_tab, interp, phase):
    box_side = vectors.shape[2]
    span = 3 * box_side
    reach = 2 * box_side - 1
    out_re = product("srcmp,sqp->srcmq", vectors[:, 0], rad_tab[:, 0]) - product(
        "srcmp,sqp->srcmq", vectors[:, 1], rad_tab[:, 1]
    )
    out_im = product("srcmp,sqp->srcmq", vectors[:, 0], rad_tab[:, 1]) + product(
        "srcmp,sqp->srcmq", vectors[:, 1], rad_tab[:, 0]
    )
    leaf_out = jnp.stack([out_re, out_im], 1)
    window = with_halo(leaf_out, (("row", 2), ("col", 3)), box_side)
    offsets = jnp.arange(2 * reach + 1) - reach
    near_offset = jnp.abs(offsets) <= 1
    keep = 1.0 - (near_offset[:, None] & near_offset[None, :]).astype(jnp.float32)
    masked = leaf_tab * keep[None, None, :, :, None]
    rows_in = []
    for row_pos in range(box_side):
        cols_in = []
        for col_pos in range(box_side):
            row_first = box_side - 1 - row_pos
            col_first = box_side - 1 - col_pos
            coeffs = masked[:, :, row_first : row_first + span, col_first : col_first + span]
            part_re, part_im = complex_mul(
                coeffs[:, 0, :, :, None], coeffs[:, 1, :, :, None], window[:, 0], window[:, 1]
            )
            cols_in.append(jnp.stack([part_re.sum((1, 2)), part_im.sum((1, 2))], 1))
        rows_in.append(jnp.stack(cols_in, 2))
    leaf_in = jnp.stack(rows_in, 2)
    interpolated = jnp.einsum("kq,sxrcmq->sxrcmk", interp, leaf_out, precision=HIGH)
    angles = phase.reshape(box_side, box_side, -1)
    cos_ph = jnp.cos(angles)[:, :, None, :]
    sin_ph = jnp.sin(angles)[:, :, None, :]
    top_re = (cos_ph * interpolated[:, 0] - sin_ph * interpolated[:, 1]).sum((1, 2))
    top_im = (cos_ph * interpolated[:, 1] + sin_ph * interpolated[:, 0]).sum((1, 2))
    top_b = jnp.stack([top_re, top_im], 1).astype(jnp.bfloat16)
    coarse_in = coarse_exchange(top_b, coarse_tab)
    in_re = coarse_in[:, 0][:, None, None]
    in_im = coarse_in[:, 1][:, None, None]
    back_re = cos_ph * in_re + sin_ph * in_im
    back_im = cos_ph * in_im - sin_ph * in_re
    spread = jnp.einsum(
        "kq,sxrcmk->sxrcmq", interp, jnp.stack([back_re, back_im], 1), precision=HIGH
    )
    incoming = (leaf_in + spread).astype(jnp.bfloat16)
    res_re = product("srcmq,spq->srcmp", incoming[:, 0], rcv_tab[:, 0]) - product(
        "srcmq,spq->srcmp", incoming[:, 1], rcv_tab[:, 1]
    )
    res_im = product("srcmq,spq->srcmp", incoming[:, 0], rcv_tab[:, 1]) + product(
        "srcmq,spq->srcmp", incoming[:, 1], rcv_tab[:, 0]
    )
    return jnp.stack([res_re, res_im], 1)


def per_device(
    current,
    probe,
    near_list,
    near_blocks,
    radiation,
    reception,
    interp,
    phase,
    leaf_table,
    coarse_table,
):
    near_fwd, near_adj = near_field(current, probe, near_list, near_blocks)
    fwd_set = (radiation, reception, leaf_table, coarse_table)
    adj_set = (
        jnp.stack([reception[0].T, -reception[1].T]),
        jnp.stack([radiation[0].T, -radiation[1].T]),
        conj_flip(leaf_table, (1, 2)),
        None,
    )
    far_both = far_field(
        jnp.stack([current, probe]),
        jnp.stack([fwd_set[0], adj_set[0]]),
        jnp.stack([fwd_set[1], adj_set[1]]),
        jnp.stack([fwd_set[2], adj_set[2]]),
        coarse_table[None],
        interp,
        phase,
    )
    far_fwd = far_both[0]
    far_adj = far_both[1]
    return (near_fwd + far_fwd, near_adj + far_adj)


def solution(mesh):
    placed = (
        P(None, "row", "col", None, None),
        P(None, "row", "col", None, None),
        P("row", "col", None),
        P(None, "row", "col", None, None, None),
        P(),
        P(),
        P(),
        P(),
        P(),
        P(),
    )
    return jax.shard_map(
        per_device,
        mesh=mesh,
        in_specs=placed,
        out_specs=(P(None, "row", "col", None, None), P(None, "row", "col", None, None)),
        check_vma=False,
    )
```

```python
import jax
import jax.numpy as jnp
from jax import lax
from jax.sharding import PartitionSpec as P

HIGH = lax.Precision.HIGHEST


def with_halo(cells, sides, width):
    for axis, dim in sides:
        count = lax.axis_size(axis)
        ends = count - 1
        head = lax.slice_in_dim(cells, 0, width, axis=dim)
        tail = lax.slice_in_dim(cells, cells.shape[dim] - width, cells.shape[dim], axis=dim)
        cells = jnp.concatenate(
            [
                lax.ppermute(tail, axis, [(i, (i + 1) % count) for i in range(ends)]),
                cells,
                lax.ppermute(head, axis, [((i + 1) % count, i) for i in range(ends)]),
            ],
            axis=dim,
        )
    return cells


def from_behind(block, axis, distance):
    devices = range(lax.axis_size(axis))
    route = [(i - distance, i) for i in devices if i - distance in devices]
    return lax.ppermute(block, axis, route)


def complex_mul(left_re, left_im, right_re, right_im):
    return (left_re * right_re - left_im * right_im, left_re * right_im + left_im * right_re)


def conj_flip(table, axes):
    flipped = jnp.flip(table, axes)
    return jnp.stack([flipped[0], -flipped[1]])


def product(form, left, right):
    return jnp.einsum(form, left, right, preferred_element_type=jnp.float32)


def near_field(current, probe, near_list, near_blocks):
    box_side = current.shape[1]
    one_hot = (near_list[..., None] == jnp.arange(9)).astype(jnp.bfloat16)
    blocks_re = near_blocks[0]
    blocks_im = near_blocks[1]
    padded = with_halo(current, (("row", 1), ("col", 2)), 1)
    shifted = jnp.stack(
        [
            padded[
                :,
                offset_code // 3 : offset_code // 3 + box_side,
                offset_code % 3 : offset_code % 3 + box_side,
            ]
            for offset_code in range(9)
        ]
    )
    picked = product("rcko,oxrcmp->xkrcmp", one_hot, shifted).astype(jnp.bfloat16)
    fwd_re = product("rckpq,krcmq->rcmp", blocks_re, picked[0]) - product(
        "rckpq,krcmq->rcmp", blocks_im, picked[1]
    )
    fwd_im = product("rckpq,krcmq->rcmp", blocks_re, picked[1]) + product(
        "rckpq,krcmq->rcmp", blocks_im, picked[0]
    )
    near_fwd = jnp.stack([fwd_re, fwd_im])
    back_re = product("rckpq,rcmp->krcmq", blocks_re, probe[0]) + product(
        "rckpq,rcmp->krcmq", blocks_im, probe[1]
    )
    back_im = product("rckpq,rcmp->krcmq", blocks_re, probe[1]) - product(
        "rckpq,rcmp->krcmq", blocks_im, probe[0]
    )
    contrib = jnp.stack([back_re, back_im])
    placed_all = jnp.einsum(
        "rcko,xkrcmp->oxrcmp", one_hot.astype(jnp.float32), contrib, precision=HIGH
    )
    placed = jnp.zeros((2, box_side + 2, box_side + 2) + contrib.shape[4:], jnp.float32)
    for offset_code in range(9):
        placed = placed.at[
            :,
            offset_code // 3 : offset_code // 3 + box_side,
            offset_code % 3 : offset_code % 3 + box_side,
        ].add(placed_all[offset_code])
    for step_dir, send_row, keep_row in ((1, box_side + 1, 1), (-1, 0, box_side)):
        arrived = from_behind(placed[:, send_row], "row", step_dir)
        placed = placed.at[:, keep_row].add(arrived)
    for step_dir, send_col, keep_col in ((1, box_side + 1, 1), (-1, 0, box_side)):
        arrived = from_behind(placed[:, 1 : box_side + 1, send_col], "col", step_dir)
        placed = placed.at[:, 1 : box_side + 1, keep_col].add(arrived)
    return (near_fwd, placed[:, 1 : box_side + 1, 1 : box_side + 1])


def gather_ordered(block, axis):
    count = lax.axis_size(axis)
    index = lax.axis_index(axis)
    held = block[None]
    step = 1
    while step < count:
        other = lax.ppermute(held, axis, [(i, i ^ step) for i in range(count)])
        lower = (index & step) == 0
        held = jnp.where(
            lower, jnp.concatenate([held, other], 0), jnp.concatenate([other, held], 0)
        )
        step *= 2
    return held


def scatter_sum(parts, axis):
    count = lax.axis_size(axis)
    index = lax.axis_index(axis)
    held = parts
    step = count // 2
    while step >= 1:
        half = held.shape[0] // 2
        upper = (index & step) != 0
        send = jnp.where(upper, held[:half], held[half:])
        keep = jnp.where(upper, held[half:], held[:half])
        held = keep + lax.ppermute(send, axis, [(i, i ^ step) for i in range(count)])
        step //= 2
    return held[0]


def coarse_exchange(top_b, coarse_tab):
    row_count = lax.axis_size("row")
    col_count = lax.axis_size("col")
    row_idx = lax.axis_index("row")
    col_idx = lax.axis_index("col")
    sources = gather_ordered(top_b, "row").astype(jnp.float32)
    zero = jnp.zeros((), jnp.int32)
    fwd_tab = coarse_tab[0]
    fwd = lax.dynamic_slice(
        fwd_tab,
        (zero, row_idx, col_count - 1 - col_idx, zero),
        (2, row_count, col_count, fwd_tab.shape[-1]),
    )
    fwd = jnp.flip(fwd, 1)
    adj = lax.dynamic_slice(
        fwd_tab,
        (zero, row_count - 1 - row_idx, col_idx, zero),
        (2, row_count, col_count, fwd_tab.shape[-1]),
    )
    adj = jnp.flip(adj, 2)
    adj = jnp.stack([adj[0], -adj[1]])
    coeff = jnp.stack([fwd, adj]).astype(jnp.float32)
    src_rows = jnp.arange(row_count)
    dst_cols = jnp.arange(col_count)
    distant = (jnp.abs(row_idx - src_rows)[:, None] > 1) | (jnp.abs(dst_cols - col_idx)[None, :] > 1)
    weight = distant.astype(jnp.float32)[None, :, :, None]
    coef_re = coeff[:, 0] * weight
    coef_im = coeff[:, 1] * weight
    val_re = jnp.moveaxis(sources[:, :, 0], 0, 1)[:, :, None]
    val_im = jnp.moveaxis(sources[:, :, 1], 0, 1)[:, :, None]
    c_re = coef_re[:, :, :, None]
    c_im = coef_im[:, :, :, None]
    got_re = (c_re * val_re - c_im * val_im).sum(1)
    got_im = (c_re * val_im + c_im * val_re).sum(1)
    parts = jnp.moveaxis(jnp.stack([got_re, got_im], 1), 2, 0)
    return scatter_sum(parts, "col")


def leaf_incoming(window, leaf_tab, box_side):
    span = 3 * box_side
    reach = 2 * box_side - 1
    width = 2 * reach + 1
    streams, _, _, _, rhs, dirs = window.shape
    targets = jnp.arange(box_side * box_side)
    cells = jnp.arange(span * span)
    d_row = (cells // span)[None, :] - (targets // box_side)[:, None] + box_side - 1
    d_col = (cells % span)[None, :] - (targets % box_side)[:, None] + box_side - 1
    far_off = (jnp.abs(d_row - reach) > 1) | (jnp.abs(d_col - reach) > 1)
    code = jnp.where(far_off, d_row * width + d_col, -1)
    pick = (code[:, :, None] == jnp.arange(width * width)).astype(jnp.float32)
    flat_tab = leaf_tab.reshape(streams, 2, width * width, dirs)
    coef = jnp.einsum("tnp,sxpq->tnsxq", pick, flat_tab, precision=HIGH)
    win = jnp.moveaxis(window, (2, 3), (0, 1)).reshape(span * span, streams, 2, rhs, dirs)
    c_re = coef[:, :, :, 0, None, :]
    c_im = coef[:, :, :, 1, None, :]
    w_re = win[None, :, :, 0]
    w_im = win[None, :, :, 1]
    in_re = (c_re * w_re - c_im * w_im).sum(1)
    in_im = (c_re * w_im + c_im * w_re).sum(1)
    leaf_in = jnp.stack([in_re, in_im], 2).reshape(box_side, box_side, streams, 2, rhs, dirs)
    return jnp.moveaxis(leaf_in, (0, 1), (2, 3))


def far_field(vectors, rad_tab, rcv_tab, leaf_tab, coarse_tab, interp, phase):
    box_side = vectors.shape[2]
    span = 3 * box_side
    reach = 2 * box_side - 1
    out_re = product("srcmp,sqp->srcmq", vectors[:, 0], rad_tab[:, 0]) - product(
        "srcmp,sqp->srcmq", vectors[:, 1], rad_tab[:, 1]
    )
    out_im = product("srcmp,sqp->srcmq", vectors[:, 0], rad_tab[:, 1]) + product(
        "srcmp,sqp->srcmq", vectors[:, 1], rad_tab[:, 0]
    )
    leaf_out = jnp.stack([out_re, out_im], 1)
    window = with_halo(leaf_out, (("row", 2), ("col", 3)), box_side)
    leaf_in = leaf_incoming(window, leaf_tab, box_side)
    interpolated = jnp.einsum("kq,sxrcmq->sxrcmk", interp, leaf_out, precision=HIGH)
    angles = phase.reshape(box_side, box_side, -1)
    cos_ph = jnp.cos(angles)[:, :, None, :]
    sin_ph = jnp.sin(angles)[:, :, None, :]
    top_re = (cos_ph * interpolated[:, 0] - sin_ph * interpolated[:, 1]).sum((1, 2))
    top_im = (cos_ph * interpolated[:, 1] + sin_ph * interpolated[:, 0]).sum((1, 2))
    top_b = jnp.stack([top_re, top_im], 1).astype(jnp.bfloat16)
    coarse_in = coarse_exchange(top_b, coarse_tab)
    in_re = coarse_in[:, 0][:, None, None]
    in_im = coarse_in[:, 1][:, None, None]
    back_re = cos_ph * in_re + sin_ph * in_im
    back_im = cos_ph * in_im - sin_ph * in_re
    spread = jnp.einsum(
        "kq,sxrcmk->sxrcmq", interp, jnp.stack([back_re, back_im], 1), precision=HIGH
    )
    incoming = (leaf_in + spread).astype(jnp.bfloat16)
    res_re = product("srcmq,spq->srcmp", incoming[:, 0], rcv_tab[:, 0]) - product(
        "srcmq,spq->srcmp", incoming[:, 1], rcv_tab[:, 1]
    )
    res_im = product("srcmq,spq->srcmp", incoming[:, 0], rcv_tab[:, 1]) + product(
        "srcmq,spq->srcmp", incoming[:, 1], rcv_tab[:, 0]
    )
    return jnp.stack([res_re, res_im], 1)


def per_device(
    current,
    probe,
    near_list,
    near_blocks,
    radiation,
    reception,
    interp,
    phase,
    leaf_table,
    coarse_table,
):
    near_fwd, near_adj = near_field(current, probe, near_list, near_blocks)
    fwd_set = (radiation, reception, leaf_table, coarse_table)
    adj_set = (
        jnp.stack([reception[0].T, -reception[1].T]),
        jnp.stack([radiation[0].T, -radiation[1].T]),
        conj_flip(leaf_table, (1, 2)),
        None,
    )
    far_both = far_field(
        jnp.stack([current, probe]),
        jnp.stack([fwd_set[0], adj_set[0]]),
        jnp.stack([fwd_set[1], adj_set[1]]),
        jnp.stack([fwd_set[2], adj_set[2]]),
        coarse_table[None],
        interp,
        phase,
    )
    far_fwd = far_both[0]
    far_adj = far_both[1]
    return (near_fwd + far_fwd, near_adj + far_adj)


def solution(mesh):
    placed = (
        P(None, "row", "col", None, None),
        P(None, "row", "col", None, None),
        P("row", "col", None),
        P(None, "row", "col", None, None, None),
        P(),
        P(),
        P(),
        P(),
        P(),
        P(),
    )
    return jax.shard_map(
        per_device,
        mesh=mesh,
        in_specs=placed,
        out_specs=(P(None, "row", "col", None, None), P(None, "row", "col", None, None)),
        check_vma=False,
    )
```

```python
import jax
import jax.numpy as jnp
from jax import lax
from jax.sharding import PartitionSpec as P

HIGH = lax.Precision.HIGHEST


def with_halo(cells, sides, width):
    for axis, dim in sides:
        count = lax.axis_size(axis)
        ends = count - 1
        head = lax.slice_in_dim(cells, 0, width, axis=dim)
        tail = lax.slice_in_dim(cells, cells.shape[dim] - width, cells.shape[dim], axis=dim)
        cells = jnp.concatenate(
            [
                lax.ppermute(tail, axis, [(i, (i + 1) % count) for i in range(ends)]),
                cells,
                lax.ppermute(head, axis, [((i + 1) % count, i) for i in range(ends)]),
            ],
            axis=dim,
        )
    return cells


def from_behind(block, axis, distance):
    devices = range(lax.axis_size(axis))
    route = [(i - distance, i) for i in devices if i - distance in devices]
    return lax.ppermute(block, axis, route)


def complex_mul(left_re, left_im, right_re, right_im):
    return (left_re * right_re - left_im * right_im, left_re * right_im + left_im * right_re)


def conj_flip(table, axes):
    flipped = jnp.flip(table, axes)
    return jnp.stack([flipped[0], -flipped[1]])


def product(form, left, right):
    return jnp.einsum(form, left, right, preferred_element_type=jnp.float32)


def near_field(current, probe, near_list, near_blocks):
    box_side = current.shape[1]
    one_hot = (near_list[..., None] == jnp.arange(9)).astype(jnp.bfloat16)
    blocks_re = near_blocks[0]
    blocks_im = near_blocks[1]
    padded = with_halo(current, (("row", 1), ("col", 2)), 1)
    shifted = jnp.stack(
        [
            padded[
                :,
                offset_code // 3 : offset_code // 3 + box_side,
                offset_code % 3 : offset_code % 3 + box_side,
            ]
            for offset_code in range(9)
        ]
    )
    picked = product("rcko,oxrcmp->xkrcmp", one_hot, shifted).astype(jnp.bfloat16)
    fwd_re = product("rckpq,krcmq->rcmp", blocks_re, picked[0]) - product(
        "rckpq,krcmq->rcmp", blocks_im, picked[1]
    )
    fwd_im = product("rckpq,krcmq->rcmp", blocks_re, picked[1]) + product(
        "rckpq,krcmq->rcmp", blocks_im, picked[0]
    )
    near_fwd = jnp.stack([fwd_re, fwd_im])
    back_re = product("rckpq,rcmp->krcmq", blocks_re, probe[0]) + product(
        "rckpq,rcmp->krcmq", blocks_im, probe[1]
    )
    back_im = product("rckpq,rcmp->krcmq", blocks_re, probe[1]) - product(
        "rckpq,rcmp->krcmq", blocks_im, probe[0]
    )
    contrib = jnp.stack([back_re, back_im])
    placed_all = jnp.einsum(
        "rcko,xkrcmp->oxrcmp", one_hot.astype(jnp.float32), contrib, precision=HIGH
    )
    placed = jnp.zeros((2, box_side + 2, box_side + 2) + contrib.shape[4:], jnp.float32)
    for offset_code in range(9):
        placed = placed.at[
            :,
            offset_code // 3 : offset_code // 3 + box_side,
            offset_code % 3 : offset_code % 3 + box_side,
        ].add(placed_all[offset_code])
    for step_dir, send_row, keep_row in ((1, box_side + 1, 1), (-1, 0, box_side)):
        arrived = from_behind(placed[:, send_row], "row", step_dir)
        placed = placed.at[:, keep_row].add(arrived)
    for step_dir, send_col, keep_col in ((1, box_side + 1, 1), (-1, 0, box_side)):
        arrived = from_behind(placed[:, 1 : box_side + 1, send_col], "col", step_dir)
        placed = placed.at[:, 1 : box_side + 1, keep_col].add(arrived)
    return (near_fwd, placed[:, 1 : box_side + 1, 1 : box_side + 1])


def gather_ordered(block, axis):
    count = lax.axis_size(axis)
    index = lax.axis_index(axis)
    held = block[None]
    step = 1
    while step < count:
        other = lax.ppermute(held, axis, [(i, i ^ step) for i in range(count)])
        lower = (index & step) == 0
        held = jnp.where(
            lower, jnp.concatenate([held, other], 0), jnp.concatenate([other, held], 0)
        )
        step *= 2
    return held


def scatter_sum(parts, axis):
    count = lax.axis_size(axis)
    index = lax.axis_index(axis)
    held = parts
    step = count // 2
    while step >= 1:
        half = held.shape[0] // 2
        upper = (index & step) != 0
        send = jnp.where(upper, held[:half], held[half:])
        keep = jnp.where(upper, held[half:], held[:half])
        held = keep + lax.ppermute(send, axis, [(i, i ^ step) for i in range(count)])
        step //= 2
    return held[0]


def gather_radix(block, axis, radix):
    count = lax.axis_size(axis)
    index = lax.axis_index(axis)
    held = block[None]
    stride = 1
    while stride < count:
        width = min(radix, count // stride)
        digit = (index // stride) % width
        pieces = [held]
        for step in range(1, width):
            pairs = [
                (i, i + (((i // stride) % width - step) % width - (i // stride) % width) * stride)
                for i in range(count)
            ]
            pieces.append(lax.ppermute(held, axis, pairs))
        ordered = jnp.roll(jnp.stack(pieces), digit, axis=0)
        held = ordered.reshape((width * held.shape[0],) + held.shape[1:])
        stride *= width
    return held


def scatter_sum_direct(parts, axis):
    count = lax.axis_size(axis)
    index = lax.axis_index(axis)
    total = lax.dynamic_index_in_dim(parts, index, 0, keepdims=False)
    for step in range(1, count):
        piece = lax.dynamic_index_in_dim(parts, (index + step) % count, 0, keepdims=False)
        total = total + lax.ppermute(piece, axis, [(i, (i + step) % count) for i in range(count)])
    return total


def coarse_exchange(top_b, coarse_tab):
    row_count = lax.axis_size("row")
    col_count = lax.axis_size("col")
    row_idx = lax.axis_index("row")
    col_idx = lax.axis_index("col")
    sources = gather_radix(top_b, "row", 8).astype(jnp.float32)
    zero = jnp.zeros((), jnp.int32)
    fwd_tab = coarse_tab[0]
    fwd = lax.dynamic_slice(
        fwd_tab,
        (zero, row_idx, col_count - 1 - col_idx, zero),
        (2, row_count, col_count, fwd_tab.shape[-1]),
    )
    fwd = jnp.flip(fwd, 1)
    adj = lax.dynamic_slice(
        fwd_tab,
        (zero, row_count - 1 - row_idx, col_idx, zero),
        (2, row_count, col_count, fwd_tab.shape[-1]),
    )
    adj = jnp.flip(adj, 2)
    adj = jnp.stack([adj[0], -adj[1]])
    coeff = jnp.stack([fwd, adj]).astype(jnp.float32)
    src_rows = jnp.arange(row_count)
    dst_cols = jnp.arange(col_count)
    distant = (jnp.abs(row_idx - src_rows)[:, None] > 1) | (jnp.abs(dst_cols - col_idx)[None, :] > 1)
    weight = distant.astype(jnp.float32)[None, :, :, None]
    coef_re = coeff[:, 0] * weight
    coef_im = coeff[:, 1] * weight
    val_re = jnp.moveaxis(sources[:, :, 0], 0, 1)[:, :, None]
    val_im = jnp.moveaxis(sources[:, :, 1], 0, 1)[:, :, None]
    c_re = coef_re[:, :, :, None]
    c_im = coef_im[:, :, :, None]
    got_re = (c_re * val_re - c_im * val_im).sum(1)
    got_im = (c_re * val_im + c_im * val_re).sum(1)
    parts = jnp.moveaxis(jnp.stack([got_re, got_im], 1), 2, 0)
    return scatter_sum_direct(parts, "col")


def leaf_incoming(window, leaf_tab, box_side):
    span = 3 * box_side
    reach = 2 * box_side - 1
    width = 2 * reach + 1
    streams, _, _, _, rhs, dirs = window.shape
    targets = jnp.arange(box_side * box_side)
    cells = jnp.arange(span * span)
    d_row = (cells // span)[None, :] - (targets // box_side)[:, None] + box_side - 1
    d_col = (cells % span)[None, :] - (targets % box_side)[:, None] + box_side - 1
    far_off = (jnp.abs(d_row - reach) > 1) | (jnp.abs(d_col - reach) > 1)
    code = jnp.where(far_off, d_row * width + d_col, -1)
    pick = (code[:, :, None] == jnp.arange(width * width)).astype(jnp.float32)
    flat_tab = leaf_tab.reshape(streams, 2, width * width, dirs)
    coef = jnp.einsum("tnp,sxpq->tnsxq", pick, flat_tab, precision=HIGH)
    win = jnp.moveaxis(window, (2, 3), (0, 1)).reshape(span * span, streams, 2, rhs, dirs)
    c_re = coef[:, :, :, 0, None, :]
    c_im = coef[:, :, :, 1, None, :]
    w_re = win[None, :, :, 0]
    w_im = win[None, :, :, 1]
    in_re = (c_re * w_re - c_im * w_im).sum(1)
    in_im = (c_re * w_im + c_im * w_re).sum(1)
    leaf_in = jnp.stack([in_re, in_im], 2).reshape(box_side, box_side, streams, 2, rhs, dirs)
    return jnp.moveaxis(leaf_in, (0, 1), (2, 3))


def far_field(vectors, rad_tab, rcv_tab, leaf_tab, coarse_tab, interp, phase):
    box_side = vectors.shape[2]
    span = 3 * box_side
    reach = 2 * box_side - 1
    out_re = product("srcmp,sqp->srcmq", vectors[:, 0], rad_tab[:, 0]) - product(
        "srcmp,sqp->srcmq", vectors[:, 1], rad_tab[:, 1]
    )
    out_im = product("srcmp,sqp->srcmq", vectors[:, 0], rad_tab[:, 1]) + product(
        "srcmp,sqp->srcmq", vectors[:, 1], rad_tab[:, 0]
    )
    leaf_out = jnp.stack([out_re, out_im], 1)
    window = with_halo(leaf_out, (("row", 2), ("col", 3)), box_side)
    leaf_in = leaf_incoming(window, leaf_tab, box_side)
    interpolated = jnp.einsum("kq,sxrcmq->sxrcmk", interp, leaf_out, precision=HIGH)
    angles = phase.reshape(box_side, box_side, -1)
    cos_ph = jnp.cos(angles)[:, :, None, :]
    sin_ph = jnp.sin(angles)[:, :, None, :]
    top_re = (cos_ph * interpolated[:, 0] - sin_ph * interpolated[:, 1]).sum((1, 2))
    top_im = (cos_ph * interpolated[:, 1] + sin_ph * interpolated[:, 0]).sum((1, 2))
    top_b = jnp.stack([top_re, top_im], 1).astype(jnp.bfloat16)
    coarse_in = coarse_exchange(top_b, coarse_tab)
    in_re = coarse_in[:, 0][:, None, None]
    in_im = coarse_in[:, 1][:, None, None]
    back_re = cos_ph * in_re + sin_ph * in_im
    back_im = cos_ph * in_im - sin_ph * in_re
    spread = jnp.einsum(
        "kq,sxrcmk->sxrcmq", interp, jnp.stack([back_re, back_im], 1), precision=HIGH
    )
    incoming = (leaf_in + spread).astype(jnp.bfloat16)
    res_re = product("srcmq,spq->srcmp", incoming[:, 0], rcv_tab[:, 0]) - product(
        "srcmq,spq->srcmp", incoming[:, 1], rcv_tab[:, 1]
    )
    res_im = product("srcmq,spq->srcmp", incoming[:, 0], rcv_tab[:, 1]) + product(
        "srcmq,spq->srcmp", incoming[:, 1], rcv_tab[:, 0]
    )
    return jnp.stack([res_re, res_im], 1)


def per_device(
    current,
    probe,
    near_list,
    near_blocks,
    radiation,
    reception,
    interp,
    phase,
    leaf_table,
    coarse_table,
):
    near_fwd, near_adj = near_field(current, probe, near_list, near_blocks)
    fwd_set = (radiation, reception, leaf_table, coarse_table)
    adj_set = (
        jnp.stack([reception[0].T, -reception[1].T]),
        jnp.stack([radiation[0].T, -radiation[1].T]),
        conj_flip(leaf_table, (1, 2)),
        None,
    )
    far_both = far_field(
        jnp.stack([current, probe]),
        jnp.stack([fwd_set[0], adj_set[0]]),
        jnp.stack([fwd_set[1], adj_set[1]]),
        jnp.stack([fwd_set[2], adj_set[2]]),
        coarse_table[None],
        interp,
        phase,
    )
    far_fwd = far_both[0]
    far_adj = far_both[1]
    return (near_fwd + far_fwd, near_adj + far_adj)


def solution(mesh):
    placed = (
        P(None, "row", "col", None, None),
        P(None, "row", "col", None, None),
        P("row", "col", None),
        P(None, "row", "col", None, None, None),
        P(),
        P(),
        P(),
        P(),
        P(),
        P(),
    )
    return jax.shard_map(
        per_device,
        mesh=mesh,
        in_specs=placed,
        out_specs=(P(None, "row", "col", None, None), P(None, "row", "col", None, None)),
        check_vma=False,
    )
```

```python
import jax
import jax.numpy as jnp
from jax import lax
from jax.sharding import PartitionSpec as P

HIGH = lax.Precision.HIGHEST


def with_halo(cells, sides, width):
    for axis, dim in sides:
        count = lax.axis_size(axis)
        ends = count - 1
        head = lax.slice_in_dim(cells, 0, width, axis=dim)
        tail = lax.slice_in_dim(cells, cells.shape[dim] - width, cells.shape[dim], axis=dim)
        cells = jnp.concatenate(
            [
                lax.ppermute(tail, axis, [(i, (i + 1) % count) for i in range(ends)]),
                cells,
                lax.ppermute(head, axis, [((i + 1) % count, i) for i in range(ends)]),
            ],
            axis=dim,
        )
    return cells


def from_behind(block, axis, distance):
    devices = range(lax.axis_size(axis))
    route = [(i - distance, i) for i in devices if i - distance in devices]
    return lax.ppermute(block, axis, route)


def complex_mul(left_re, left_im, right_re, right_im):
    return (left_re * right_re - left_im * right_im, left_re * right_im + left_im * right_re)


def conj_flip(table, axes):
    flipped = jnp.flip(table, axes)
    return jnp.stack([flipped[0], -flipped[1]])


def product(form, left, right):
    return jnp.einsum(form, left, right, preferred_element_type=jnp.float32)


def near_field(padded, current, probe, near_list, near_blocks):
    box_side = current.shape[1]
    one_hot = (near_list[..., None] == jnp.arange(9)).astype(jnp.bfloat16)
    blocks_re = near_blocks[0]
    blocks_im = near_blocks[1]
    shifted = jnp.stack(
        [
            padded[
                :,
                offset_code // 3 : offset_code // 3 + box_side,
                offset_code % 3 : offset_code % 3 + box_side,
            ]
            for offset_code in range(9)
        ]
    )
    picked = product("rcko,oxrcmp->xkrcmp", one_hot, shifted).astype(jnp.bfloat16)
    fwd_re = product("rckpq,krcmq->rcmp", blocks_re, picked[0]) - product(
        "rckpq,krcmq->rcmp", blocks_im, picked[1]
    )
    fwd_im = product("rckpq,krcmq->rcmp", blocks_re, picked[1]) + product(
        "rckpq,krcmq->rcmp", blocks_im, picked[0]
    )
    near_fwd = jnp.stack([fwd_re, fwd_im])
    back_re = product("rckpq,rcmp->krcmq", blocks_re, probe[0]) + product(
        "rckpq,rcmp->krcmq", blocks_im, probe[1]
    )
    back_im = product("rckpq,rcmp->krcmq", blocks_re, probe[1]) - product(
        "rckpq,rcmp->krcmq", blocks_im, probe[0]
    )
    contrib = jnp.stack([back_re, back_im])
    placed_all = jnp.einsum(
        "rcko,xkrcmp->oxrcmp", one_hot.astype(jnp.float32), contrib, precision=HIGH
    )
    placed = jnp.zeros((2, box_side + 2, box_side + 2) + contrib.shape[4:], jnp.float32)
    for offset_code in range(9):
        placed = placed.at[
            :,
            offset_code // 3 : offset_code // 3 + box_side,
            offset_code % 3 : offset_code % 3 + box_side,
        ].add(placed_all[offset_code])
    for step_dir, send_row, keep_row in ((1, box_side + 1, 1), (-1, 0, box_side)):
        arrived = from_behind(placed[:, send_row], "row", step_dir)
        placed = placed.at[:, keep_row].add(arrived)
    for step_dir, send_col, keep_col in ((1, box_side + 1, 1), (-1, 0, box_side)):
        arrived = from_behind(placed[:, 1 : box_side + 1, send_col], "col", step_dir)
        placed = placed.at[:, 1 : box_side + 1, keep_col].add(arrived)
    return (near_fwd, placed[:, 1 : box_side + 1, 1 : box_side + 1])


def gather_ordered(block, axis):
    count = lax.axis_size(axis)
    index = lax.axis_index(axis)
    held = block[None]
    step = 1
    while step < count:
        other = lax.ppermute(held, axis, [(i, i ^ step) for i in range(count)])
        lower = (index & step) == 0
        held = jnp.where(
            lower, jnp.concatenate([held, other], 0), jnp.concatenate([other, held], 0)
        )
        step *= 2
    return held


def scatter_sum(parts, axis):
    count = lax.axis_size(axis)
    index = lax.axis_index(axis)
    held = parts
    step = count // 2
    while step >= 1:
        half = held.shape[0] // 2
        upper = (index & step) != 0
        send = jnp.where(upper, held[:half], held[half:])
        keep = jnp.where(upper, held[half:], held[:half])
        held = keep + lax.ppermute(send, axis, [(i, i ^ step) for i in range(count)])
        step //= 2
    return held[0]


def coarse_exchange(top_b, coarse_tab):
    row_count = lax.axis_size("row")
    col_count = lax.axis_size("col")
    row_idx = lax.axis_index("row")
    col_idx = lax.axis_index("col")
    sources = gather_ordered(top_b, "row").astype(jnp.float32)
    zero = jnp.zeros((), jnp.int32)
    fwd_tab = coarse_tab[0]
    fwd = lax.dynamic_slice(
        fwd_tab,
        (zero, row_idx, col_count - 1 - col_idx, zero),
        (2, row_count, col_count, fwd_tab.shape[-1]),
    )
    fwd = jnp.flip(fwd, 1)
    adj = lax.dynamic_slice(
        fwd_tab,
        (zero, row_count - 1 - row_idx, col_idx, zero),
        (2, row_count, col_count, fwd_tab.shape[-1]),
    )
    adj = jnp.flip(adj, 2)
    adj = jnp.stack([adj[0], -adj[1]])
    coeff = jnp.stack([fwd, adj]).astype(jnp.float32)
    src_rows = jnp.arange(row_count)
    dst_cols = jnp.arange(col_count)
    distant = (jnp.abs(row_idx - src_rows)[:, None] > 1) | (jnp.abs(dst_cols - col_idx)[None, :] > 1)
    weight = distant.astype(jnp.float32)[None, :, :, None]
    coef_re = coeff[:, 0] * weight
    coef_im = coeff[:, 1] * weight
    val_re = jnp.moveaxis(sources[:, :, 0], 0, 1)[:, :, None]
    val_im = jnp.moveaxis(sources[:, :, 1], 0, 1)[:, :, None]
    c_re = coef_re[:, :, :, None]
    c_im = coef_im[:, :, :, None]
    got_re = (c_re * val_re - c_im * val_im).sum(1)
    got_im = (c_re * val_im + c_im * val_re).sum(1)
    parts = jnp.moveaxis(jnp.stack([got_re, got_im], 1), 2, 0)
    return scatter_sum(parts, "col")


def leaf_incoming(window, leaf_tab, box_side):
    span = 3 * box_side
    reach = 2 * box_side - 1
    width = 2 * reach + 1
    streams, _, _, _, rhs, dirs = window.shape
    targets = jnp.arange(box_side * box_side)
    cells = jnp.arange(span * span)
    d_row = (cells // span)[None, :] - (targets // box_side)[:, None] + box_side - 1
    d_col = (cells % span)[None, :] - (targets % box_side)[:, None] + box_side - 1
    far_off = (jnp.abs(d_row - reach) > 1) | (jnp.abs(d_col - reach) > 1)
    code = jnp.where(far_off, d_row * width + d_col, -1)
    pick = (code[:, :, None] == jnp.arange(width * width)).astype(jnp.float32)
    flat_tab = leaf_tab.reshape(streams, 2, width * width, dirs)
    coef = jnp.einsum("tnp,sxpq->tnsxq", pick, flat_tab, precision=HIGH)
    win = jnp.moveaxis(window, (2, 3), (0, 1)).reshape(span * span, streams, 2, rhs, dirs)
    c_re = coef[:, :, :, 0, None, :]
    c_im = coef[:, :, :, 1, None, :]
    w_re = win[None, :, :, 0]
    w_im = win[None, :, :, 1]
    in_re = (c_re * w_re - c_im * w_im).sum(1)
    in_im = (c_re * w_im + c_im * w_re).sum(1)
    leaf_in = jnp.stack([in_re, in_im], 2).reshape(box_side, box_side, streams, 2, rhs, dirs)
    return jnp.moveaxis(leaf_in, (0, 1), (2, 3))


def far_field(vectors, rad_tab, rcv_tab, leaf_tab, coarse_tab, interp, phase):
    box_side = vectors.shape[2] // 3
    span = 3 * box_side
    reach = 2 * box_side - 1
    out_re = product("srcmp,sqp->srcmq", vectors[:, 0], rad_tab[:, 0]) - product(
        "srcmp,sqp->srcmq", vectors[:, 1], rad_tab[:, 1]
    )
    out_im = product("srcmp,sqp->srcmq", vectors[:, 0], rad_tab[:, 1]) + product(
        "srcmp,sqp->srcmq", vectors[:, 1], rad_tab[:, 0]
    )
    window = jnp.stack([out_re, out_im], 1)
    leaf_out = window[:, :, box_side : 2 * box_side, box_side : 2 * box_side]
    leaf_in = leaf_incoming(window, leaf_tab, box_side)
    interpolated = jnp.einsum("kq,sxrcmq->sxrcmk", interp, leaf_out, precision=HIGH)
    angles = phase.reshape(box_side, box_side, -1)
    cos_ph = jnp.cos(angles)[:, :, None, :]
    sin_ph = jnp.sin(angles)[:, :, None, :]
    top_re = (cos_ph * interpolated[:, 0] - sin_ph * interpolated[:, 1]).sum((1, 2))
    top_im = (cos_ph * interpolated[:, 1] + sin_ph * interpolated[:, 0]).sum((1, 2))
    top_b = jnp.stack([top_re, top_im], 1).astype(jnp.bfloat16)
    coarse_in = coarse_exchange(top_b, coarse_tab)
    in_re = coarse_in[:, 0][:, None, None]
    in_im = coarse_in[:, 1][:, None, None]
    back_re = cos_ph * in_re + sin_ph * in_im
    back_im = cos_ph * in_im - sin_ph * in_re
    spread = jnp.einsum(
        "kq,sxrcmk->sxrcmq", interp, jnp.stack([back_re, back_im], 1), precision=HIGH
    )
    incoming = (leaf_in + spread).astype(jnp.bfloat16)
    res_re = product("srcmq,spq->srcmp", incoming[:, 0], rcv_tab[:, 0]) - product(
        "srcmq,spq->srcmp", incoming[:, 1], rcv_tab[:, 1]
    )
    res_im = product("srcmq,spq->srcmp", incoming[:, 0], rcv_tab[:, 1]) + product(
        "srcmq,spq->srcmp", incoming[:, 1], rcv_tab[:, 0]
    )
    return jnp.stack([res_re, res_im], 1)


def per_device(
    current,
    probe,
    near_list,
    near_blocks,
    radiation,
    reception,
    interp,
    phase,
    leaf_table,
    coarse_table,
):
    box_side = current.shape[1]
    vectors = with_halo(jnp.stack([current, probe]), (("row", 2), ("col", 3)), box_side)
    padded = vectors[0][:, box_side - 1 : 2 * box_side + 1, box_side - 1 : 2 * box_side + 1]
    near_fwd, near_adj = near_field(padded, current, probe, near_list, near_blocks)
    fwd_set = (radiation, reception, leaf_table, coarse_table)
    adj_set = (
        jnp.stack([reception[0].T, -reception[1].T]),
        jnp.stack([radiation[0].T, -radiation[1].T]),
        conj_flip(leaf_table, (1, 2)),
        None,
    )
    far_both = far_field(
        vectors,
        jnp.stack([fwd_set[0], adj_set[0]]),
        jnp.stack([fwd_set[1], adj_set[1]]),
        jnp.stack([fwd_set[2], adj_set[2]]),
        coarse_table[None],
        interp,
        phase,
    )
    far_fwd = far_both[0]
    far_adj = far_both[1]
    return (near_fwd + far_fwd, near_adj + far_adj)


def solution(mesh):
    placed = (
        P(None, "row", "col", None, None),
        P(None, "row", "col", None, None),
        P("row", "col", None),
        P(None, "row", "col", None, None, None),
        P(),
        P(),
        P(),
        P(),
        P(),
        P(),
    )
    return jax.shard_map(
        per_device,
        mesh=mesh,
        in_specs=placed,
        out_specs=(P(None, "row", "col", None, None), P(None, "row", "col", None, None)),
        check_vma=False,
    )
```

```python
import jax
import jax.numpy as jnp
from jax import lax
from jax.sharding import PartitionSpec as P

HIGH = lax.Precision.HIGHEST


def with_halo(cells, sides, width):
    for axis, dim in sides:
        count = lax.axis_size(axis)
        ends = count - 1
        head = lax.slice_in_dim(cells, 0, width, axis=dim)
        tail = lax.slice_in_dim(cells, cells.shape[dim] - width, cells.shape[dim], axis=dim)
        cells = jnp.concatenate(
            [
                lax.ppermute(tail, axis, [(i, (i + 1) % count) for i in range(ends)]),
                cells,
                lax.ppermute(head, axis, [((i + 1) % count, i) for i in range(ends)]),
            ],
            axis=dim,
        )
    return cells


def from_behind(block, axis, distance):
    devices = range(lax.axis_size(axis))
    route = [(i - distance, i) for i in devices if i - distance in devices]
    return lax.ppermute(block, axis, route)


def complex_mul(left_re, left_im, right_re, right_im):
    return (left_re * right_re - left_im * right_im, left_re * right_im + left_im * right_re)


def conj_flip(table, axes):
    flipped = jnp.flip(table, axes)
    return jnp.stack([flipped[0], -flipped[1]])


def product(form, left, right):
    return jnp.einsum(form, left, right, preferred_element_type=jnp.float32)


def near_forward(padded, near_list, near_blocks):
    box_side = padded.shape[1] - 2
    one_hot = (near_list[..., None] == jnp.arange(9)).astype(jnp.bfloat16)
    blocks_re = near_blocks[0]
    blocks_im = near_blocks[1]
    shifted = jnp.stack(
        [
            padded[
                :,
                offset_code // 3 : offset_code // 3 + box_side,
                offset_code % 3 : offset_code % 3 + box_side,
            ]
            for offset_code in range(9)
        ]
    )
    picked = product("rcko,oxrcmp->xkrcmp", one_hot, shifted).astype(jnp.bfloat16)
    fwd_re = product("rckpq,krcmq->rcmp", blocks_re, picked[0]) - product(
        "rckpq,krcmq->rcmp", blocks_im, picked[1]
    )
    fwd_im = product("rckpq,krcmq->rcmp", blocks_re, picked[1]) + product(
        "rckpq,krcmq->rcmp", blocks_im, picked[0]
    )
    return jnp.stack([fwd_re, fwd_im])


def near_adjoint_local(probe, near_list, near_blocks):
    box_side = probe.shape[1]
    one_hot = (near_list[..., None] == jnp.arange(9)).astype(jnp.bfloat16)
    blocks_re = near_blocks[0]
    blocks_im = near_blocks[1]
    back_re = product("rckpq,rcmp->krcmq", blocks_re, probe[0]) + product(
        "rckpq,rcmp->krcmq", blocks_im, probe[1]
    )
    back_im = product("rckpq,rcmp->krcmq", blocks_re, probe[1]) - product(
        "rckpq,rcmp->krcmq", blocks_im, probe[0]
    )
    contrib = jnp.stack([back_re, back_im])
    placed_all = jnp.einsum(
        "rcko,xkrcmp->oxrcmp", one_hot.astype(jnp.float32), contrib, precision=HIGH
    )
    placed = jnp.zeros((2, box_side + 2, box_side + 2) + contrib.shape[4:], jnp.float32)
    for offset_code in range(9):
        placed = placed.at[
            :,
            offset_code // 3 : offset_code // 3 + box_side,
            offset_code % 3 : offset_code % 3 + box_side,
        ].add(placed_all[offset_code])
    return placed


def exchange_halo(vectors, placed):
    box_side = vectors.shape[2]
    lanes = vectors.shape[-1]
    cells = vectors.astype(jnp.float32)
    for axis, dim in (("row", 2), ("col", 3)):
        count = lax.axis_size(axis)
        ahead = [(i, i + 1) for i in range(count - 1)]
        behind = [(i + 1, i) for i in range(count - 1)]
        flat = cells.reshape(-1, lanes)
        size = flat.shape[0]
        if axis == "row":
            to_next = placed[:, box_side + 1]
            to_prev = placed[:, 0]
        else:
            to_next = placed[:, 1 : box_side + 1, box_side + 1]
            to_prev = placed[:, 1 : box_side + 1, 0]
        edge_shape = to_next.shape
        from_prev = lax.ppermute(
            jnp.concatenate([flat, to_next.reshape(-1, lanes)]), axis, ahead
        )
        from_next = lax.ppermute(
            jnp.concatenate([flat, to_prev.reshape(-1, lanes)]), axis, behind
        )
        if axis == "row":
            placed = placed.at[:, 1].add(from_prev[size:].reshape(edge_shape))
            placed = placed.at[:, box_side].add(from_next[size:].reshape(edge_shape))
        else:
            placed = placed.at[:, 1 : box_side + 1, 1].add(from_prev[size:].reshape(edge_shape))
            placed = placed.at[:, 1 : box_side + 1, box_side].add(
                from_next[size:].reshape(edge_shape)
            )
        cells = jnp.concatenate(
            [from_prev[:size].reshape(cells.shape), cells, from_next[:size].reshape(cells.shape)],
            axis=dim,
        )
    return cells.astype(jnp.bfloat16), placed[:, 1 : box_side + 1, 1 : box_side + 1]


def gather_ordered(block, axis):
    count = lax.axis_size(axis)
    index = lax.axis_index(axis)
    held = block[None]
    step = 1
    while step < count:
        other = lax.ppermute(held, axis, [(i, i ^ step) for i in range(count)])
        lower = (index & step) == 0
        held = jnp.where(
            lower, jnp.concatenate([held, other], 0), jnp.concatenate([other, held], 0)
        )
        step *= 2
    return held


def scatter_sum(parts, axis):
    count = lax.axis_size(axis)
    index = lax.axis_index(axis)
    held = parts
    step = count // 2
    while step >= 1:
        half = held.shape[0] // 2
        upper = (index & step) != 0
        send = jnp.where(upper, held[:half], held[half:])
        keep = jnp.where(upper, held[half:], held[:half])
        held = keep + lax.ppermute(send, axis, [(i, i ^ step) for i in range(count)])
        step //= 2
    return held[0]


def coarse_exchange(top_b, coarse_tab):
    row_count = lax.axis_size("row")
    col_count = lax.axis_size("col")
    row_idx = lax.axis_index("row")
    col_idx = lax.axis_index("col")
    sources = gather_ordered(top_b, "row").astype(jnp.float32)
    zero = jnp.zeros((), jnp.int32)
    fwd_tab = coarse_tab[0]
    fwd = lax.dynamic_slice(
        fwd_tab,
        (zero, row_idx, col_count - 1 - col_idx, zero),
        (2, row_count, col_count, fwd_tab.shape[-1]),
    )
    fwd = jnp.flip(fwd, 1)
    adj = lax.dynamic_slice(
        fwd_tab,
        (zero, row_count - 1 - row_idx, col_idx, zero),
        (2, row_count, col_count, fwd_tab.shape[-1]),
    )
    adj = jnp.flip(adj, 2)
    adj = jnp.stack([adj[0], -adj[1]])
    coeff = jnp.stack([fwd, adj]).astype(jnp.float32)
    src_rows = jnp.arange(row_count)
    dst_cols = jnp.arange(col_count)
    distant = (jnp.abs(row_idx - src_rows)[:, None] > 1) | (jnp.abs(dst_cols - col_idx)[None, :] > 1)
    weight = distant.astype(jnp.float32)[None, :, :, None]
    coef_re = coeff[:, 0] * weight
    coef_im = coeff[:, 1] * weight
    val_re = jnp.moveaxis(sources[:, :, 0], 0, 1)[:, :, None]
    val_im = jnp.moveaxis(sources[:, :, 1], 0, 1)[:, :, None]
    c_re = coef_re[:, :, :, None]
    c_im = coef_im[:, :, :, None]
    got_re = (c_re * val_re - c_im * val_im).sum(1)
    got_im = (c_re * val_im + c_im * val_re).sum(1)
    parts = jnp.moveaxis(jnp.stack([got_re, got_im], 1), 2, 0)
    return scatter_sum(parts, "col")


def leaf_incoming(window, leaf_tab, box_side):
    span = 3 * box_side
    reach = 2 * box_side - 1
    width = 2 * reach + 1
    streams, _, _, _, rhs, dirs = window.shape
    targets = jnp.arange(box_side * box_side)
    cells = jnp.arange(span * span)
    d_row = (cells // span)[None, :] - (targets // box_side)[:, None] + box_side - 1
    d_col = (cells % span)[None, :] - (targets % box_side)[:, None] + box_side - 1
    far_off = (jnp.abs(d_row - reach) > 1) | (jnp.abs(d_col - reach) > 1)
    code = jnp.where(far_off, d_row * width + d_col, -1)
    pick = (code[:, :, None] == jnp.arange(width * width)).astype(jnp.float32)
    flat_tab = leaf_tab.reshape(streams, 2, width * width, dirs)
    coef = jnp.einsum("tnp,sxpq->tnsxq", pick, flat_tab, precision=HIGH)
    win = jnp.moveaxis(window, (2, 3), (0, 1)).reshape(span * span, streams, 2, rhs, dirs)
    c_re = coef[:, :, :, 0, None, :]
    c_im = coef[:, :, :, 1, None, :]
    w_re = win[None, :, :, 0]
    w_im = win[None, :, :, 1]
    in_re = (c_re * w_re - c_im * w_im).sum(1)
    in_im = (c_re * w_im + c_im * w_re).sum(1)
    leaf_in = jnp.stack([in_re, in_im], 2).reshape(box_side, box_side, streams, 2, rhs, dirs)
    return jnp.moveaxis(leaf_in, (0, 1), (2, 3))


def far_field(vectors, rad_tab, rcv_tab, leaf_tab, coarse_tab, interp, phase):
    box_side = vectors.shape[2] // 3
    span = 3 * box_side
    reach = 2 * box_side - 1
    out_re = product("srcmp,sqp->srcmq", vectors[:, 0], rad_tab[:, 0]) - product(
        "srcmp,sqp->srcmq", vectors[:, 1], rad_tab[:, 1]
    )
    out_im = product("srcmp,sqp->srcmq", vectors[:, 0], rad_tab[:, 1]) + product(
        "srcmp,sqp->srcmq", vectors[:, 1], rad_tab[:, 0]
    )
    window = jnp.stack([out_re, out_im], 1)
    leaf_out = window[:, :, box_side : 2 * box_side, box_side : 2 * box_side]
    leaf_in = leaf_incoming(window, leaf_tab, box_side)
    interpolated = jnp.einsum("kq,sxrcmq->sxrcmk", interp, leaf_out, precision=HIGH)
    angles = phase.reshape(box_side, box_side, -1)
    cos_ph = jnp.cos(angles)[:, :, None, :]
    sin_ph = jnp.sin(angles)[:, :, None, :]
    top_re = (cos_ph * interpolated[:, 0] - sin_ph * interpolated[:, 1]).sum((1, 2))
    top_im = (cos_ph * interpolated[:, 1] + sin_ph * interpolated[:, 0]).sum((1, 2))
    top_b = jnp.stack([top_re, top_im], 1).astype(jnp.bfloat16)
    coarse_in = coarse_exchange(top_b, coarse_tab)
    in_re = coarse_in[:, 0][:, None, None]
    in_im = coarse_in[:, 1][:, None, None]
    back_re = cos_ph * in_re + sin_ph * in_im
    back_im = cos_ph * in_im - sin_ph * in_re
    spread = jnp.einsum(
        "kq,sxrcmk->sxrcmq", interp, jnp.stack([back_re, back_im], 1), precision=HIGH
    )
    incoming = (leaf_in + spread).astype(jnp.bfloat16)
    res_re = product("srcmq,spq->srcmp", incoming[:, 0], rcv_tab[:, 0]) - product(
        "srcmq,spq->srcmp", incoming[:, 1], rcv_tab[:, 1]
    )
    res_im = product("srcmq,spq->srcmp", incoming[:, 0], rcv_tab[:, 1]) + product(
        "srcmq,spq->srcmp", incoming[:, 1], rcv_tab[:, 0]
    )
    return jnp.stack([res_re, res_im], 1)


def per_device(
    current,
    probe,
    near_list,
    near_blocks,
    radiation,
    reception,
    interp,
    phase,
    leaf_table,
    coarse_table,
):
    box_side = current.shape[1]
    placed = near_adjoint_local(probe, near_list, near_blocks)
    vectors, near_adj = exchange_halo(jnp.stack([current, probe]), placed)
    padded = vectors[0][:, box_side - 1 : 2 * box_side + 1, box_side - 1 : 2 * box_side + 1]
    near_fwd = near_forward(padded, near_list, near_blocks)
    fwd_set = (radiation, reception, leaf_table, coarse_table)
    adj_set = (
        jnp.stack([reception[0].T, -reception[1].T]),
        jnp.stack([radiation[0].T, -radiation[1].T]),
        conj_flip(leaf_table, (1, 2)),
        None,
    )
    far_both = far_field(
        vectors,
        jnp.stack([fwd_set[0], adj_set[0]]),
        jnp.stack([fwd_set[1], adj_set[1]]),
        jnp.stack([fwd_set[2], adj_set[2]]),
        coarse_table[None],
        interp,
        phase,
    )
    far_fwd = far_both[0]
    far_adj = far_both[1]
    return (near_fwd + far_fwd, near_adj + far_adj)


def solution(mesh):
    placed = (
        P(None, "row", "col", None, None),
        P(None, "row", "col", None, None),
        P("row", "col", None),
        P(None, "row", "col", None, None, None),
        P(),
        P(),
        P(),
        P(),
        P(),
        P(),
    )
    return jax.shard_map(
        per_device,
        mesh=mesh,
        in_specs=placed,
        out_specs=(P(None, "row", "col", None, None), P(None, "row", "col", None, None)),
        check_vma=False,
    )
```

```python
import jax
import jax.numpy as jnp
from jax import lax
from jax.sharding import PartitionSpec as P

HIGH = lax.Precision.HIGHEST


def with_halo(cells, sides, width):
    for axis, dim in sides:
        count = lax.axis_size(axis)
        ends = count - 1
        head = lax.slice_in_dim(cells, 0, width, axis=dim)
        tail = lax.slice_in_dim(cells, cells.shape[dim] - width, cells.shape[dim], axis=dim)
        cells = jnp.concatenate(
            [
                lax.ppermute(tail, axis, [(i, (i + 1) % count) for i in range(ends)]),
                cells,
                lax.ppermute(head, axis, [((i + 1) % count, i) for i in range(ends)]),
            ],
            axis=dim,
        )
    return cells


def from_behind(block, axis, distance):
    devices = range(lax.axis_size(axis))
    route = [(i - distance, i) for i in devices if i - distance in devices]
    return lax.ppermute(block, axis, route)


def complex_mul(left_re, left_im, right_re, right_im):
    return (left_re * right_re - left_im * right_im, left_re * right_im + left_im * right_re)


def conj_flip(table, axes):
    flipped = jnp.flip(table, axes)
    return jnp.stack([flipped[0], -flipped[1]])


def product(form, left, right):
    return jnp.einsum(form, left, right, preferred_element_type=jnp.float32)


def near_forward(padded, near_list, near_blocks):
    box_side = padded.shape[1] - 2
    one_hot = (near_list[..., None] == jnp.arange(9)).astype(jnp.bfloat16)
    blocks_re = near_blocks[0]
    blocks_im = near_blocks[1]
    shifted = jnp.stack(
        [
            padded[
                :,
                offset_code // 3 : offset_code // 3 + box_side,
                offset_code % 3 : offset_code % 3 + box_side,
            ]
            for offset_code in range(9)
        ]
    )
    picked = product("rcko,oxrcmp->xkrcmp", one_hot, shifted).astype(jnp.bfloat16)
    fwd_re = product("rckpq,krcmq->rcmp", blocks_re, picked[0]) - product(
        "rckpq,krcmq->rcmp", blocks_im, picked[1]
    )
    fwd_im = product("rckpq,krcmq->rcmp", blocks_re, picked[1]) + product(
        "rckpq,krcmq->rcmp", blocks_im, picked[0]
    )
    return jnp.stack([fwd_re, fwd_im])


def near_adjoint_local(probe, near_list, near_blocks):
    box_side = probe.shape[1]
    one_hot = (near_list[..., None] == jnp.arange(9)).astype(jnp.bfloat16)
    blocks_re = near_blocks[0]
    blocks_im = near_blocks[1]
    back_re = product("rckpq,rcmp->krcmq", blocks_re, probe[0]) + product(
        "rckpq,rcmp->krcmq", blocks_im, probe[1]
    )
    back_im = product("rckpq,rcmp->krcmq", blocks_re, probe[1]) - product(
        "rckpq,rcmp->krcmq", blocks_im, probe[0]
    )
    contrib = jnp.stack([back_re, back_im])
    placed_all = jnp.einsum(
        "rcko,xkrcmp->oxrcmp", one_hot.astype(jnp.float32), contrib, precision=HIGH
    )
    placed = jnp.zeros((2, box_side + 2, box_side + 2) + contrib.shape[4:], jnp.float32)
    for offset_code in range(9):
        placed = placed.at[
            :,
            offset_code // 3 : offset_code // 3 + box_side,
            offset_code % 3 : offset_code % 3 + box_side,
        ].add(placed_all[offset_code])
    return placed


def exchange_halo(vectors, placed):
    box_side = vectors.shape[2]
    lanes = vectors.shape[-1]
    cells = vectors.astype(jnp.float32)
    for axis, dim in (("row", 2), ("col", 3)):
        count = lax.axis_size(axis)
        ahead = [(i, i + 1) for i in range(count - 1)]
        behind = [(i + 1, i) for i in range(count - 1)]
        flat = cells.reshape(-1, lanes)
        size = flat.shape[0]
        if axis == "row":
            to_next = placed[:, box_side + 1]
            to_prev = placed[:, 0]
        else:
            to_next = placed[:, 1 : box_side + 1, box_side + 1]
            to_prev = placed[:, 1 : box_side + 1, 0]
        edge_shape = to_next.shape
        from_prev = lax.ppermute(
            jnp.concatenate([flat, to_next.reshape(-1, lanes)]), axis, ahead
        )
        from_next = lax.ppermute(
            jnp.concatenate([flat, to_prev.reshape(-1, lanes)]), axis, behind
        )
        if axis == "row":
            placed = placed.at[:, 1].add(from_prev[size:].reshape(edge_shape))
            placed = placed.at[:, box_side].add(from_next[size:].reshape(edge_shape))
        else:
            placed = placed.at[:, 1 : box_side + 1, 1].add(from_prev[size:].reshape(edge_shape))
            placed = placed.at[:, 1 : box_side + 1, box_side].add(
                from_next[size:].reshape(edge_shape)
            )
        cells = jnp.concatenate(
            [from_prev[:size].reshape(cells.shape), cells, from_next[:size].reshape(cells.shape)],
            axis=dim,
        )
    return cells.astype(jnp.bfloat16), placed[:, 1 : box_side + 1, 1 : box_side + 1]


def gather_ordered(block, axis):
    count = lax.axis_size(axis)
    index = lax.axis_index(axis)
    held = block[None]
    step = 1
    while step < count:
        other = lax.ppermute(held, axis, [(i, i ^ step) for i in range(count)])
        lower = (index & step) == 0
        held = jnp.where(
            lower, jnp.concatenate([held, other], 0), jnp.concatenate([other, held], 0)
        )
        step *= 2
    return held


def scatter_sum(parts, axis):
    count = lax.axis_size(axis)
    index = lax.axis_index(axis)
    held = parts
    step = count // 2
    while step >= 1:
        half = held.shape[0] // 2
        upper = (index & step) != 0
        send = jnp.where(upper, held[:half], held[half:])
        keep = jnp.where(upper, held[half:], held[:half])
        held = keep + lax.ppermute(send, axis, [(i, i ^ step) for i in range(count)])
        step //= 2
    return held[0]


def coarse_exchange(top_b, coarse_tab):
    row_count = lax.axis_size("row")
    col_count = lax.axis_size("col")
    row_idx = lax.axis_index("row")
    col_idx = lax.axis_index("col")
    sources = gather_ordered(top_b, "row").astype(jnp.float32)
    zero = jnp.zeros((), jnp.int32)
    fwd_tab = coarse_tab[0]
    fwd = lax.dynamic_slice(
        fwd_tab,
        (zero, row_idx, col_count - 1 - col_idx, zero),
        (2, row_count, col_count, fwd_tab.shape[-1]),
    )
    fwd = jnp.flip(fwd, 1)
    adj = lax.dynamic_slice(
        fwd_tab,
        (zero, row_count - 1 - row_idx, col_idx, zero),
        (2, row_count, col_count, fwd_tab.shape[-1]),
    )
    adj = jnp.flip(adj, 2)
    adj = jnp.stack([adj[0], -adj[1]])
    coeff = jnp.stack([fwd, adj]).astype(jnp.float32)
    src_rows = jnp.arange(row_count)
    dst_cols = jnp.arange(col_count)
    distant = (jnp.abs(row_idx - src_rows)[:, None] > 1) | (jnp.abs(dst_cols - col_idx)[None, :] > 1)
    weight = distant.astype(jnp.float32)[None, :, :, None]
    coef_re = coeff[:, 0] * weight
    coef_im = coeff[:, 1] * weight
    val_re = jnp.moveaxis(sources[:, :, 0], 0, 1)[:, :, None]
    val_im = jnp.moveaxis(sources[:, :, 1], 0, 1)[:, :, None]
    c_re = coef_re[:, :, :, None]
    c_im = coef_im[:, :, :, None]
    got_re = (c_re * val_re - c_im * val_im).sum(1)
    got_im = (c_re * val_im + c_im * val_re).sum(1)
    parts = jnp.moveaxis(jnp.stack([got_re, got_im], 1), 2, 0)
    return scatter_sum(parts, "col")


def leaf_incoming(window, leaf_tab, box_side):
    span = 3 * box_side
    reach = 2 * box_side - 1
    width = 2 * reach + 1
    streams, _, _, _, rhs, dirs = window.shape
    targets = jnp.arange(box_side * box_side)
    cells = jnp.arange(span * span)
    d_row = (cells // span)[None, :] - (targets // box_side)[:, None] + box_side - 1
    d_col = (cells % span)[None, :] - (targets % box_side)[:, None] + box_side - 1
    far_off = (jnp.abs(d_row - reach) > 1) | (jnp.abs(d_col - reach) > 1)
    code = jnp.where(far_off, d_row * width + d_col, -1)
    pick = (code[:, :, None] == jnp.arange(width * width)).astype(jnp.float32)
    flat_tab = leaf_tab.reshape(streams, 2, width * width, dirs)
    coef = jnp.einsum("tnp,sxpq->tnsxq", pick, flat_tab, precision=HIGH)
    win = jnp.moveaxis(window, (2, 3), (0, 1)).reshape(span * span, streams, 2, rhs, dirs)
    c_re = coef[:, :, :, 0, None, :]
    c_im = coef[:, :, :, 1, None, :]
    w_re = win[None, :, :, 0]
    w_im = win[None, :, :, 1]
    in_re = (c_re * w_re - c_im * w_im).sum(1)
    in_im = (c_re * w_im + c_im * w_re).sum(1)
    leaf_in = jnp.stack([in_re, in_im], 2).reshape(box_side, box_side, streams, 2, rhs, dirs)
    return jnp.moveaxis(leaf_in, (0, 1), (2, 3))


def radiate(vectors, rad_tab):
    out_re = product("srcmp,sqp->srcmq", vectors[:, 0], rad_tab[:, 0]) - product(
        "srcmp,sqp->srcmq", vectors[:, 1], rad_tab[:, 1]
    )
    out_im = product("srcmp,sqp->srcmq", vectors[:, 0], rad_tab[:, 1]) + product(
        "srcmp,sqp->srcmq", vectors[:, 1], rad_tab[:, 0]
    )
    return jnp.stack([out_re, out_im], 1)


def far_field(own, vectors, rad_tab, rcv_tab, leaf_tab, coarse_tab, interp, phase):
    box_side = own.shape[2]
    span = 3 * box_side
    reach = 2 * box_side - 1
    leaf_out = radiate(own, rad_tab)
    window = radiate(vectors, rad_tab)
    leaf_in = leaf_incoming(window, leaf_tab, box_side)
    interpolated = jnp.einsum("kq,sxrcmq->sxrcmk", interp, leaf_out, precision=HIGH)
    angles = phase.reshape(box_side, box_side, -1)
    cos_ph = jnp.cos(angles)[:, :, None, :]
    sin_ph = jnp.sin(angles)[:, :, None, :]
    top_re = (cos_ph * interpolated[:, 0] - sin_ph * interpolated[:, 1]).sum((1, 2))
    top_im = (cos_ph * interpolated[:, 1] + sin_ph * interpolated[:, 0]).sum((1, 2))
    top_b = jnp.stack([top_re, top_im], 1).astype(jnp.bfloat16)
    coarse_in = coarse_exchange(top_b, coarse_tab)
    in_re = coarse_in[:, 0][:, None, None]
    in_im = coarse_in[:, 1][:, None, None]
    back_re = cos_ph * in_re + sin_ph * in_im
    back_im = cos_ph * in_im - sin_ph * in_re
    spread = jnp.einsum(
        "kq,sxrcmk->sxrcmq", interp, jnp.stack([back_re, back_im], 1), precision=HIGH
    )
    incoming = (leaf_in + spread).astype(jnp.bfloat16)
    res_re = product("srcmq,spq->srcmp", incoming[:, 0], rcv_tab[:, 0]) - product(
        "srcmq,spq->srcmp", incoming[:, 1], rcv_tab[:, 1]
    )
    res_im = product("srcmq,spq->srcmp", incoming[:, 0], rcv_tab[:, 1]) + product(
        "srcmq,spq->srcmp", incoming[:, 1], rcv_tab[:, 0]
    )
    return jnp.stack([res_re, res_im], 1)


def per_device(
    current,
    probe,
    near_list,
    near_blocks,
    radiation,
    reception,
    interp,
    phase,
    leaf_table,
    coarse_table,
):
    box_side = current.shape[1]
    placed = near_adjoint_local(probe, near_list, near_blocks)
    vectors, near_adj = exchange_halo(jnp.stack([current, probe]), placed)
    padded = vectors[0][:, box_side - 1 : 2 * box_side + 1, box_side - 1 : 2 * box_side + 1]
    near_fwd = near_forward(padded, near_list, near_blocks)
    fwd_set = (radiation, reception, leaf_table, coarse_table)
    adj_set = (
        jnp.stack([reception[0].T, -reception[1].T]),
        jnp.stack([radiation[0].T, -radiation[1].T]),
        conj_flip(leaf_table, (1, 2)),
        None,
    )
    far_both = far_field(
        jnp.stack([current, probe]),
        vectors,
        jnp.stack([fwd_set[0], adj_set[0]]),
        jnp.stack([fwd_set[1], adj_set[1]]),
        jnp.stack([fwd_set[2], adj_set[2]]),
        coarse_table[None],
        interp,
        phase,
    )
    far_fwd = far_both[0]
    far_adj = far_both[1]
    return (near_fwd + far_fwd, near_adj + far_adj)


def solution(mesh):
    placed = (
        P(None, "row", "col", None, None),
        P(None, "row", "col", None, None),
        P("row", "col", None),
        P(None, "row", "col", None, None, None),
        P(),
        P(),
        P(),
        P(),
        P(),
        P(),
    )
    return jax.shard_map(
        per_device,
        mesh=mesh,
        in_specs=placed,
        out_specs=(P(None, "row", "col", None, None), P(None, "row", "col", None, None)),
        check_vma=False,
    )
```

```python
import jax
import jax.numpy as jnp
from jax import lax
from jax.sharding import PartitionSpec as P

HIGH = lax.Precision.HIGHEST


def with_halo(cells, sides, width):
    for axis, dim in sides:
        count = lax.axis_size(axis)
        ends = count - 1
        head = lax.slice_in_dim(cells, 0, width, axis=dim)
        tail = lax.slice_in_dim(cells, cells.shape[dim] - width, cells.shape[dim], axis=dim)
        cells = jnp.concatenate(
            [
                lax.ppermute(tail, axis, [(i, (i + 1) % count) for i in range(ends)]),
                cells,
                lax.ppermute(head, axis, [((i + 1) % count, i) for i in range(ends)]),
            ],
            axis=dim,
        )
    return cells


def from_behind(block, axis, distance):
    devices = range(lax.axis_size(axis))
    route = [(i - distance, i) for i in devices if i - distance in devices]
    return lax.ppermute(block, axis, route)


def complex_mul(left_re, left_im, right_re, right_im):
    return (left_re * right_re - left_im * right_im, left_re * right_im + left_im * right_re)


def conj_flip(table, axes):
    flipped = jnp.flip(table, axes)
    return jnp.stack([flipped[0], -flipped[1]])


def product(form, left, right):
    return jnp.einsum(form, left, right, preferred_element_type=jnp.float32)


def near_forward(padded, near_list, near_blocks):
    box_side = padded.shape[1] - 2
    one_hot = (near_list[..., None] == jnp.arange(9)).astype(jnp.bfloat16)
    blocks_re = near_blocks[0]
    blocks_im = near_blocks[1]
    shifted = jnp.stack(
        [
            padded[
                :,
                offset_code // 3 : offset_code // 3 + box_side,
                offset_code % 3 : offset_code % 3 + box_side,
            ]
            for offset_code in range(9)
        ]
    )
    picked = product("rcko,oxrcmp->xkrcmp", one_hot, shifted).astype(jnp.bfloat16)
    fwd_re = product("rckpq,krcmq->rcmp", blocks_re, picked[0]) - product(
        "rckpq,krcmq->rcmp", blocks_im, picked[1]
    )
    fwd_im = product("rckpq,krcmq->rcmp", blocks_re, picked[1]) + product(
        "rckpq,krcmq->rcmp", blocks_im, picked[0]
    )
    return jnp.stack([fwd_re, fwd_im])


def near_adjoint_local(probe, near_list, near_blocks):
    box_side = probe.shape[1]
    one_hot = (near_list[..., None] == jnp.arange(9)).astype(jnp.bfloat16)
    blocks_re = near_blocks[0]
    blocks_im = near_blocks[1]
    back_re = product("rckpq,rcmp->krcmq", blocks_re, probe[0]) + product(
        "rckpq,rcmp->krcmq", blocks_im, probe[1]
    )
    back_im = product("rckpq,rcmp->krcmq", blocks_re, probe[1]) - product(
        "rckpq,rcmp->krcmq", blocks_im, probe[0]
    )
    contrib = jnp.stack([back_re, back_im])
    placed_all = jnp.einsum(
        "rcko,xkrcmp->oxrcmp", one_hot.astype(jnp.float32), contrib, precision=HIGH
    )
    placed = jnp.zeros((2, box_side + 2, box_side + 2) + contrib.shape[4:], jnp.float32)
    for offset_code in range(9):
        placed = placed.at[
            :,
            offset_code // 3 : offset_code // 3 + box_side,
            offset_code % 3 : offset_code % 3 + box_side,
        ].add(placed_all[offset_code])
    return placed


def exchange_halo(vectors, placed):
    box_side = vectors.shape[2]
    lanes = vectors.shape[-1]
    cells = vectors.astype(jnp.float32)
    for axis, dim in (("row", 2), ("col", 3)):
        count = lax.axis_size(axis)
        ahead = [(i, i + 1) for i in range(count - 1)]
        behind = [(i + 1, i) for i in range(count - 1)]
        flat = cells.reshape(-1, lanes)
        size = flat.shape[0]
        if axis == "row":
            to_next = placed[:, box_side + 1]
            to_prev = placed[:, 0]
        else:
            to_next = placed[:, 1 : box_side + 1, box_side + 1]
            to_prev = placed[:, 1 : box_side + 1, 0]
        edge_shape = to_next.shape
        from_prev = lax.ppermute(
            jnp.concatenate([flat, to_next.reshape(-1, lanes)]), axis, ahead
        )
        from_next = lax.ppermute(
            jnp.concatenate([flat, to_prev.reshape(-1, lanes)]), axis, behind
        )
        if axis == "row":
            placed = placed.at[:, 1].add(from_prev[size:].reshape(edge_shape))
            placed = placed.at[:, box_side].add(from_next[size:].reshape(edge_shape))
        else:
            placed = placed.at[:, 1 : box_side + 1, 1].add(from_prev[size:].reshape(edge_shape))
            placed = placed.at[:, 1 : box_side + 1, box_side].add(
                from_next[size:].reshape(edge_shape)
            )
        cells = jnp.concatenate(
            [from_prev[:size].reshape(cells.shape), cells, from_next[:size].reshape(cells.shape)],
            axis=dim,
        )
    return cells.astype(jnp.bfloat16), placed[:, 1 : box_side + 1, 1 : box_side + 1]


def step_order(count):
    minor = 16 if count % 16 == 0 else count
    steps = [1 << b for b in range(count.bit_length() - 1)]
    low = [k for k in steps if k < minor]
    high = [k for k in steps if k >= minor]
    return low[::-1] + high[::-1]


def gather_ordered(block, axis):
    count = lax.axis_size(axis)
    index = lax.axis_index(axis)
    held = block[None]
    steps = step_order(count)
    for step in steps:
        other = lax.ppermute(held, axis, [(i, i ^ step) for i in range(count)])
        lower = (index & step) == 0
        held = jnp.where(
            lower, jnp.concatenate([held, other], 0), jnp.concatenate([other, held], 0)
        )
    bits = len(steps)
    exps = [step.bit_length() - 1 for step in steps]
    perm = [bits - 1 - exps.index(e) for e in range(bits - 1, -1, -1)]
    held = held.reshape((2,) * bits + held.shape[1:])
    held = jnp.transpose(held, perm + list(range(bits, held.ndim)))
    return held.reshape((count,) + block.shape)


def scatter_sum(parts, axis):
    count = lax.axis_size(axis)
    index = lax.axis_index(axis)
    bits = count.bit_length() - 1
    held = parts.reshape((2,) * bits + parts.shape[1:])
    remaining = list(range(bits - 1, -1, -1))
    for exp in range(bits):
        step = 1 << exp
        at = remaining.index(exp)
        upper = (index & step) != 0
        lo = lax.index_in_dim(held, 0, at, keepdims=False)
        hi = lax.index_in_dim(held, 1, at, keepdims=False)
        send = jnp.where(upper, lo, hi)
        keep = jnp.where(upper, hi, lo)
        held = keep + lax.ppermute(send, axis, [(i, i ^ step) for i in range(count)])
        remaining.pop(at)
    return held


def coarse_exchange(top_b, coarse_tab):
    row_count = lax.axis_size("row")
    col_count = lax.axis_size("col")
    row_idx = lax.axis_index("row")
    col_idx = lax.axis_index("col")
    sources = gather_ordered(top_b, "row").astype(jnp.float32)
    zero = jnp.zeros((), jnp.int32)
    fwd_tab = coarse_tab[0]
    fwd = lax.dynamic_slice(
        fwd_tab,
        (zero, row_idx, col_count - 1 - col_idx, zero),
        (2, row_count, col_count, fwd_tab.shape[-1]),
    )
    fwd = jnp.flip(fwd, 1)
    adj = lax.dynamic_slice(
        fwd_tab,
        (zero, row_count - 1 - row_idx, col_idx, zero),
        (2, row_count, col_count, fwd_tab.shape[-1]),
    )
    adj = jnp.flip(adj, 2)
    adj = jnp.stack([adj[0], -adj[1]])
    coeff = jnp.stack([fwd, adj]).astype(jnp.float32)
    src_rows = jnp.arange(row_count)
    dst_cols = jnp.arange(col_count)
    distant = (jnp.abs(row_idx - src_rows)[:, None] > 1) | (jnp.abs(dst_cols - col_idx)[None, :] > 1)
    weight = distant.astype(jnp.float32)[None, :, :, None]
    coef_re = coeff[:, 0] * weight
    coef_im = coeff[:, 1] * weight
    val_re = jnp.moveaxis(sources[:, :, 0], 0, 1)[:, :, None]
    val_im = jnp.moveaxis(sources[:, :, 1], 0, 1)[:, :, None]
    c_re = coef_re[:, :, :, None]
    c_im = coef_im[:, :, :, None]
    got_re = (c_re * val_re - c_im * val_im).sum(1)
    got_im = (c_re * val_im + c_im * val_re).sum(1)
    parts = jnp.moveaxis(jnp.stack([got_re, got_im], 1), 2, 0)
    return scatter_sum(parts, "col")


def leaf_incoming(window, leaf_tab, box_side):
    span = 3 * box_side
    reach = 2 * box_side - 1
    width = 2 * reach + 1
    streams, _, _, _, rhs, dirs = window.shape
    targets = jnp.arange(box_side * box_side)
    cells = jnp.arange(span * span)
    d_row = (cells // span)[None, :] - (targets // box_side)[:, None] + box_side - 1
    d_col = (cells % span)[None, :] - (targets % box_side)[:, None] + box_side - 1
    far_off = (jnp.abs(d_row - reach) > 1) | (jnp.abs(d_col - reach) > 1)
    code = jnp.where(far_off, d_row * width + d_col, -1)
    pick = (code[:, :, None] == jnp.arange(width * width)).astype(jnp.float32)
    flat_tab = leaf_tab.reshape(streams, 2, width * width, dirs)
    coef = jnp.einsum("tnp,sxpq->tnsxq", pick, flat_tab, precision=HIGH)
    win = jnp.moveaxis(window, (2, 3), (0, 1)).reshape(span * span, streams, 2, rhs, dirs)
    c_re = coef[:, :, :, 0, None, :]
    c_im = coef[:, :, :, 1, None, :]
    w_re = win[None, :, :, 0]
    w_im = win[None, :, :, 1]
    in_re = (c_re * w_re - c_im * w_im).sum(1)
    in_im = (c_re * w_im + c_im * w_re).sum(1)
    leaf_in = jnp.stack([in_re, in_im], 2).reshape(box_side, box_side, streams, 2, rhs, dirs)
    return jnp.moveaxis(leaf_in, (0, 1), (2, 3))


def radiate(vectors, rad_tab):
    out_re = product("srcmp,sqp->srcmq", vectors[:, 0], rad_tab[:, 0]) - product(
        "srcmp,sqp->srcmq", vectors[:, 1], rad_tab[:, 1]
    )
    out_im = product("srcmp,sqp->srcmq", vectors[:, 0], rad_tab[:, 1]) + product(
        "srcmp,sqp->srcmq", vectors[:, 1], rad_tab[:, 0]
    )
    return jnp.stack([out_re, out_im], 1)


def far_field(own, vectors, rad_tab, rcv_tab, leaf_tab, coarse_tab, interp, phase):
    box_side = own.shape[2]
    span = 3 * box_side
    reach = 2 * box_side - 1
    leaf_out = radiate(own, rad_tab)
    window = radiate(vectors, rad_tab)
    leaf_in = leaf_incoming(window, leaf_tab, box_side)
    interpolated = jnp.einsum("kq,sxrcmq->sxrcmk", interp, leaf_out, precision=HIGH)
    angles = phase.reshape(box_side, box_side, -1)
    cos_ph = jnp.cos(angles)[:, :, None, :]
    sin_ph = jnp.sin(angles)[:, :, None, :]
    top_re = (cos_ph * interpolated[:, 0] - sin_ph * interpolated[:, 1]).sum((1, 2))
    top_im = (cos_ph * interpolated[:, 1] + sin_ph * interpolated[:, 0]).sum((1, 2))
    top_b = jnp.stack([top_re, top_im], 1).astype(jnp.bfloat16)
    coarse_in = coarse_exchange(top_b, coarse_tab)
    in_re = coarse_in[:, 0][:, None, None]
    in_im = coarse_in[:, 1][:, None, None]
    back_re = cos_ph * in_re + sin_ph * in_im
    back_im = cos_ph * in_im - sin_ph * in_re
    spread = jnp.einsum(
        "kq,sxrcmk->sxrcmq", interp, jnp.stack([back_re, back_im], 1), precision=HIGH
    )
    incoming = (leaf_in + spread).astype(jnp.bfloat16)
    res_re = product("srcmq,spq->srcmp", incoming[:, 0], rcv_tab[:, 0]) - product(
        "srcmq,spq->srcmp", incoming[:, 1], rcv_tab[:, 1]
    )
    res_im = product("srcmq,spq->srcmp", incoming[:, 0], rcv_tab[:, 1]) + product(
        "srcmq,spq->srcmp", incoming[:, 1], rcv_tab[:, 0]
    )
    return jnp.stack([res_re, res_im], 1)


def per_device(
    current,
    probe,
    near_list,
    near_blocks,
    radiation,
    reception,
    interp,
    phase,
    leaf_table,
    coarse_table,
):
    box_side = current.shape[1]
    placed = near_adjoint_local(probe, near_list, near_blocks)
    vectors, near_adj = exchange_halo(jnp.stack([current, probe]), placed)
    padded = vectors[0][:, box_side - 1 : 2 * box_side + 1, box_side - 1 : 2 * box_side + 1]
    near_fwd = near_forward(padded, near_list, near_blocks)
    fwd_set = (radiation, reception, leaf_table, coarse_table)
    adj_set = (
        jnp.stack([reception[0].T, -reception[1].T]),
        jnp.stack([radiation[0].T, -radiation[1].T]),
        conj_flip(leaf_table, (1, 2)),
        None,
    )
    far_both = far_field(
        jnp.stack([current, probe]),
        vectors,
        jnp.stack([fwd_set[0], adj_set[0]]),
        jnp.stack([fwd_set[1], adj_set[1]]),
        jnp.stack([fwd_set[2], adj_set[2]]),
        coarse_table[None],
        interp,
        phase,
    )
    far_fwd = far_both[0]
    far_adj = far_both[1]
    return (near_fwd + far_fwd, near_adj + far_adj)


def solution(mesh):
    placed = (
        P(None, "row", "col", None, None),
        P(None, "row", "col", None, None),
        P("row", "col", None),
        P(None, "row", "col", None, None, None),
        P(),
        P(),
        P(),
        P(),
        P(),
        P(),
    )
    return jax.shard_map(
        per_device,
        mesh=mesh,
        in_specs=placed,
        out_specs=(P(None, "row", "col", None, None), P(None, "row", "col", None, None)),
        check_vma=False,
    )
```

```python
import jax
import jax.numpy as jnp
from jax import lax
from jax.sharding import PartitionSpec as P

HIGH = lax.Precision.HIGHEST


def conj_flip(table, axes):
    flipped = jnp.flip(table, axes)
    return jnp.stack([flipped[0], -flipped[1]])


def product(form, left, right):
    return jnp.einsum(form, left, right, preferred_element_type=jnp.float32)


def near_forward(padded, near_list, near_blocks):
    box_side = padded.shape[1] - 2
    one_hot = (near_list[..., None] == jnp.arange(9)).astype(jnp.bfloat16)
    blocks_re = near_blocks[0]
    blocks_im = near_blocks[1]
    shifted = jnp.stack(
        [
            padded[
                :,
                offset_code // 3 : offset_code // 3 + box_side,
                offset_code % 3 : offset_code % 3 + box_side,
            ]
            for offset_code in range(9)
        ]
    )
    picked = product("rcko,oxrcmp->xkrcmp", one_hot, shifted).astype(jnp.bfloat16)
    fwd_re = product("rckpq,krcmq->rcmp", blocks_re, picked[0]) - product(
        "rckpq,krcmq->rcmp", blocks_im, picked[1]
    )
    fwd_im = product("rckpq,krcmq->rcmp", blocks_re, picked[1]) + product(
        "rckpq,krcmq->rcmp", blocks_im, picked[0]
    )
    return jnp.stack([fwd_re, fwd_im])


def near_adjoint_local(probe, near_list, near_blocks):
    box_side = probe.shape[1]
    one_hot = (near_list[..., None] == jnp.arange(9)).astype(jnp.bfloat16)
    blocks_re = near_blocks[0]
    blocks_im = near_blocks[1]
    back_re = product("rckpq,rcmp->krcmq", blocks_re, probe[0]) + product(
        "rckpq,rcmp->krcmq", blocks_im, probe[1]
    )
    back_im = product("rckpq,rcmp->krcmq", blocks_re, probe[1]) - product(
        "rckpq,rcmp->krcmq", blocks_im, probe[0]
    )
    contrib = jnp.stack([back_re, back_im])
    placed_all = jnp.einsum(
        "rcko,xkrcmp->oxrcmp", one_hot.astype(jnp.float32), contrib, precision=HIGH
    )
    placed = jnp.zeros((2, box_side + 2, box_side + 2) + contrib.shape[4:], jnp.float32)
    for offset_code in range(9):
        placed = placed.at[
            :,
            offset_code // 3 : offset_code // 3 + box_side,
            offset_code % 3 : offset_code % 3 + box_side,
        ].add(placed_all[offset_code])
    return placed


def exchange_halo(vectors, placed):
    box_side = vectors.shape[2]
    lanes = vectors.shape[-1]
    cells = vectors.astype(jnp.float32)
    for axis, dim in (("row", 2), ("col", 3)):
        count = lax.axis_size(axis)
        ahead = [(i, i + 1) for i in range(count - 1)]
        behind = [(i + 1, i) for i in range(count - 1)]
        flat = cells.reshape(-1, lanes)
        size = flat.shape[0]
        if axis == "row":
            to_next = placed[:, box_side + 1]
            to_prev = placed[:, 0]
        else:
            to_next = placed[:, 1 : box_side + 1, box_side + 1]
            to_prev = placed[:, 1 : box_side + 1, 0]
        edge_shape = to_next.shape
        from_prev = lax.ppermute(jnp.concatenate([flat, to_next.reshape(-1, lanes)]), axis, ahead)
        from_next = lax.ppermute(jnp.concatenate([flat, to_prev.reshape(-1, lanes)]), axis, behind)
        if axis == "row":
            placed = placed.at[:, 1].add(from_prev[size:].reshape(edge_shape))
            placed = placed.at[:, box_side].add(from_next[size:].reshape(edge_shape))
        else:
            placed = placed.at[:, 1 : box_side + 1, 1].add(from_prev[size:].reshape(edge_shape))
            placed = placed.at[:, 1 : box_side + 1, box_side].add(
                from_next[size:].reshape(edge_shape)
            )
        cells = jnp.concatenate(
            [from_prev[:size].reshape(cells.shape), cells, from_next[:size].reshape(cells.shape)],
            axis=dim,
        )
    return cells.astype(jnp.bfloat16), placed[:, 1 : box_side + 1, 1 : box_side + 1]


def step_order(count):
    minor = 16 if count % 16 == 0 else count
    steps = [1 << b for b in range(count.bit_length() - 1)]
    low = [k for k in steps if k < minor]
    high = [k for k in steps if k >= minor]
    return low[::-1] + high[::-1]


def scatter_sum(parts, axis):
    count = lax.axis_size(axis)
    index = lax.axis_index(axis)
    bits = count.bit_length() - 1
    held = parts.reshape((2,) * bits + parts.shape[1:])
    remaining = list(range(bits - 1, -1, -1))
    for exp in range(bits):
        step = 1 << exp
        at = remaining.index(exp)
        upper = (index & step) != 0
        lo = lax.index_in_dim(held, 0, at, keepdims=False)
        hi = lax.index_in_dim(held, 1, at, keepdims=False)
        send = jnp.where(upper, lo, hi)
        keep = jnp.where(upper, hi, lo)
        held = keep + lax.ppermute(send, axis, [(i, i ^ step) for i in range(count)])
        remaining.pop(at)
    return held


def gather_halves(block, axis):
    count = lax.axis_size(axis)
    index = lax.axis_index(axis)
    held = block[None]
    steps = step_order(count)
    for step in steps[:-1]:
        other = lax.ppermute(held, axis, [(i, i ^ step) for i in range(count)])
        lower = (index & step) == 0
        held = jnp.where(
            lower, jnp.concatenate([held, other], 0), jnp.concatenate([other, held], 0)
        )
    bits = len(steps) - 1
    exps = [step.bit_length() - 1 for step in steps[:-1]]
    order = sorted(exps, reverse=True)
    perm = [bits - 1 - exps.index(e) for e in order]
    held = held.reshape((2,) * bits + held.shape[1:])
    held = jnp.transpose(held, perm + list(range(bits, held.ndim)))
    held = held.reshape((count // 2,) + block.shape)
    last = steps[-1]
    other = lax.ppermute(held, axis, [(i, i ^ last) for i in range(count)])
    return held, other, last


def coarse_exchange(top_b, coarse_tab):
    row_count = lax.axis_size("row")
    col_count = lax.axis_size("col")
    row_idx = lax.axis_index("row")
    col_idx = lax.axis_index("col")
    mine, theirs, last = gather_halves(top_b, "row")
    zero = jnp.zeros((), jnp.int32)
    fwd_tab = coarse_tab[0]
    fwd = lax.dynamic_slice(
        fwd_tab,
        (zero, row_idx, col_count - 1 - col_idx, zero),
        (2, row_count, col_count, fwd_tab.shape[-1]),
    )
    fwd = jnp.flip(fwd, 1)
    adj = lax.dynamic_slice(
        fwd_tab,
        (zero, row_count - 1 - row_idx, col_idx, zero),
        (2, row_count, col_count, fwd_tab.shape[-1]),
    )
    adj = jnp.flip(adj, 2)
    adj = jnp.stack([adj[0], -adj[1]])
    coeff = jnp.stack([fwd, adj]).astype(jnp.float32)
    src_rows = jnp.arange(row_count)
    dst_cols = jnp.arange(col_count)
    distant = (jnp.abs(row_idx - src_rows)[:, None] > 1) | (jnp.abs(dst_cols - col_idx)[None, :] > 1)
    weight = distant.astype(jnp.float32)[None, :, :, None]
    coef_re = coeff[:, 0] * weight
    coef_im = coeff[:, 1] * weight
    own_bit = (row_idx // last) % 2

    def half(coef, bit):
        shape = coef.shape
        coef = coef.reshape((shape[0], row_count // (2 * last), 2, last) + shape[2:])
        coef = lax.dynamic_index_in_dim(coef, bit, 2, keepdims=False)
        return coef.reshape((shape[0], row_count // 2) + shape[2:])[:, :, :, None]

    def partial(sources, c_re, c_im):
        sources = sources.astype(jnp.float32)
        val_re = jnp.moveaxis(sources[:, :, 0], 0, 1)[:, :, None]
        val_im = jnp.moveaxis(sources[:, :, 1], 0, 1)[:, :, None]
        return (c_re * val_re - c_im * val_im).sum(1), (c_re * val_im + c_im * val_re).sum(1)

    near_re, near_im = partial(mine, half(coef_re, own_bit), half(coef_im, own_bit))
    far_re, far_im = partial(theirs, half(coef_re, 1 - own_bit), half(coef_im, 1 - own_bit))
    got_re = near_re + far_re
    got_im = near_im + far_im
    parts = jnp.moveaxis(jnp.stack([got_re, got_im], 1), 2, 0)
    return scatter_sum(parts, "col")


def leaf_incoming(window, leaf_tab, box_side):
    span = 3 * box_side
    reach = 2 * box_side - 1
    width = 2 * reach + 1
    streams, _, _, _, rhs, dirs = window.shape
    targets = jnp.arange(box_side * box_side)
    cells = jnp.arange(span * span)
    d_row = (cells // span)[None, :] - (targets // box_side)[:, None] + box_side - 1
    d_col = (cells % span)[None, :] - (targets % box_side)[:, None] + box_side - 1
    far_off = (jnp.abs(d_row - reach) > 1) | (jnp.abs(d_col - reach) > 1)
    code = jnp.where(far_off, d_row * width + d_col, -1)
    pick = (code[:, :, None] == jnp.arange(width * width)).astype(jnp.float32)
    flat_tab = leaf_tab.reshape(streams, 2, width * width, dirs)
    coef = jnp.einsum("tnp,sxpq->tnsxq", pick, flat_tab, precision=HIGH)
    win = jnp.moveaxis(window, (2, 3), (0, 1)).reshape(span * span, streams, 2, rhs, dirs)
    c_re = coef[:, :, :, 0, None, :]
    c_im = coef[:, :, :, 1, None, :]
    w_re = win[None, :, :, 0]
    w_im = win[None, :, :, 1]
    in_re = (c_re * w_re - c_im * w_im).sum(1)
    in_im = (c_re * w_im + c_im * w_re).sum(1)
    leaf_in = jnp.stack([in_re, in_im], 2).reshape(box_side, box_side, streams, 2, rhs, dirs)
    return jnp.moveaxis(leaf_in, (0, 1), (2, 3))


def radiate(vectors, rad_tab):
    out_re = product("srcmp,sqp->srcmq", vectors[:, 0], rad_tab[:, 0]) - product(
        "srcmp,sqp->srcmq", vectors[:, 1], rad_tab[:, 1]
    )
    out_im = product("srcmp,sqp->srcmq", vectors[:, 0], rad_tab[:, 1]) + product(
        "srcmp,sqp->srcmq", vectors[:, 1], rad_tab[:, 0]
    )
    return jnp.stack([out_re, out_im], 1)


def far_field(own, vectors, rad_tab, rcv_tab, leaf_tab, coarse_tab, interp, phase):
    box_side = own.shape[2]
    leaf_out = radiate(own, rad_tab)
    window = radiate(vectors, rad_tab)
    leaf_in = leaf_incoming(window, leaf_tab, box_side)
    interpolated = jnp.einsum("kq,sxrcmq->sxrcmk", interp, leaf_out, precision=HIGH)
    angles = phase.reshape(box_side, box_side, -1)
    cos_ph = jnp.cos(angles)[:, :, None, :]
    sin_ph = jnp.sin(angles)[:, :, None, :]
    top_re = (cos_ph * interpolated[:, 0] - sin_ph * interpolated[:, 1]).sum((1, 2))
    top_im = (cos_ph * interpolated[:, 1] + sin_ph * interpolated[:, 0]).sum((1, 2))
    top_b = jnp.stack([top_re, top_im], 1).astype(jnp.bfloat16)
    coarse_in = coarse_exchange(top_b, coarse_tab)
    in_re = coarse_in[:, 0][:, None, None]
    in_im = coarse_in[:, 1][:, None, None]
    back_re = cos_ph * in_re + sin_ph * in_im
    back_im = cos_ph * in_im - sin_ph * in_re
    spread = jnp.einsum(
        "kq,sxrcmk->sxrcmq", interp, jnp.stack([back_re, back_im], 1), precision=HIGH
    )
    incoming = (leaf_in + spread).astype(jnp.bfloat16)
    res_re = product("srcmq,spq->srcmp", incoming[:, 0], rcv_tab[:, 0]) - product(
        "srcmq,spq->srcmp", incoming[:, 1], rcv_tab[:, 1]
    )
    res_im = product("srcmq,spq->srcmp", incoming[:, 0], rcv_tab[:, 1]) + product(
        "srcmq,spq->srcmp", incoming[:, 1], rcv_tab[:, 0]
    )
    return jnp.stack([res_re, res_im], 1)


def per_device_body(
    current,
    probe,
    near_list,
    near_blocks,
    radiation,
    reception,
    interp,
    phase,
    leaf_table,
    coarse_table,
):
    box_side = current.shape[1]
    placed = near_adjoint_local(probe, near_list, near_blocks)
    vectors, near_adj = exchange_halo(jnp.stack([current, probe]), placed)
    padded = vectors[0][:, box_side - 1 : 2 * box_side + 1, box_side - 1 : 2 * box_side + 1]
    near_fwd = near_forward(padded, near_list, near_blocks)
    fwd_set = (radiation, reception, leaf_table, coarse_table)
    adj_set = (
        jnp.stack([reception[0].T, -reception[1].T]),
        jnp.stack([radiation[0].T, -radiation[1].T]),
        conj_flip(leaf_table, (1, 2)),
        None,
    )
    far_both = far_field(
        jnp.stack([current, probe]),
        vectors,
        jnp.stack([fwd_set[0], adj_set[0]]),
        jnp.stack([fwd_set[1], adj_set[1]]),
        jnp.stack([fwd_set[2], adj_set[2]]),
        coarse_table[None],
        interp,
        phase,
    )
    far_fwd = far_both[0]
    far_adj = far_both[1]
    return (near_fwd + far_fwd, near_adj + far_adj)


def solution(mesh):
    placed = (
        P(None, "row", "col", None, None),
        P(None, "row", "col", None, None),
        P("row", "col", None),
        P(None, "row", "col", None, None, None),
        P(),
        P(),
        P(),
        P(),
        P(),
        P(),
    )
    return jax.shard_map(
        per_device_body,
        mesh=mesh,
        in_specs=placed,
        out_specs=(P(None, "row", "col", None, None), P(None, "row", "col", None, None)),
        check_vma=False,
    )
```

```python
import jax
import jax.numpy as jnp
from jax import lax
from jax.sharding import PartitionSpec as P

HIGH = lax.Precision.HIGHEST


def conj_flip(table, axes):
    flipped = jnp.flip(table, axes)
    return jnp.stack([flipped[0], -flipped[1]])


def product(form, left, right):
    return jnp.einsum(form, left, right, preferred_element_type=jnp.float32)


def near_forward(padded, near_list, near_blocks):
    box_side = padded.shape[1] - 2
    one_hot = (near_list[..., None] == jnp.arange(9)).astype(jnp.bfloat16)
    blocks_re = near_blocks[0]
    blocks_im = near_blocks[1]
    shifted = jnp.stack(
        [
            padded[
                :,
                offset_code // 3 : offset_code // 3 + box_side,
                offset_code % 3 : offset_code % 3 + box_side,
            ]
            for offset_code in range(9)
        ]
    )
    picked = product("rcko,oxrcmp->xkrcmp", one_hot, shifted).astype(jnp.bfloat16)
    fwd_re = product("rckpq,krcmq->rcmp", blocks_re, picked[0]) - product(
        "rckpq,krcmq->rcmp", blocks_im, picked[1]
    )
    fwd_im = product("rckpq,krcmq->rcmp", blocks_re, picked[1]) + product(
        "rckpq,krcmq->rcmp", blocks_im, picked[0]
    )
    return jnp.stack([fwd_re, fwd_im])


def near_adjoint_local(probe, near_list, near_blocks):
    box_side = probe.shape[1]
    one_hot = (near_list[..., None] == jnp.arange(9)).astype(jnp.bfloat16)
    blocks_re = near_blocks[0]
    blocks_im = near_blocks[1]
    back_re = product("rckpq,rcmp->krcmq", blocks_re, probe[0]) + product(
        "rckpq,rcmp->krcmq", blocks_im, probe[1]
    )
    back_im = product("rckpq,rcmp->krcmq", blocks_re, probe[1]) - product(
        "rckpq,rcmp->krcmq", blocks_im, probe[0]
    )
    contrib = jnp.stack([back_re, back_im])
    placed_all = jnp.einsum(
        "rcko,xkrcmp->oxrcmp", one_hot.astype(jnp.float32), contrib, precision=HIGH
    )
    placed = jnp.zeros((2, box_side + 2, box_side + 2) + contrib.shape[4:], jnp.float32)
    for offset_code in range(9):
        placed = placed.at[
            :,
            offset_code // 3 : offset_code // 3 + box_side,
            offset_code % 3 : offset_code % 3 + box_side,
        ].add(placed_all[offset_code])
    return placed


def exchange_halo(vectors, placed):
    box_side = vectors.shape[2]
    lanes = vectors.shape[-1]
    cells = vectors.astype(jnp.float32)
    for axis, dim in (("row", 2), ("col", 3)):
        count = lax.axis_size(axis)
        ahead = [(i, i + 1) for i in range(count - 1)]
        behind = [(i + 1, i) for i in range(count - 1)]
        flat = cells.reshape(-1, lanes)
        size = flat.shape[0]
        if axis == "row":
            to_next = placed[:, box_side + 1]
            to_prev = placed[:, 0]
        else:
            to_next = placed[:, 1 : box_side + 1, box_side + 1]
            to_prev = placed[:, 1 : box_side + 1, 0]
        edge_shape = to_next.shape
        from_prev = lax.ppermute(jnp.concatenate([flat, to_next.reshape(-1, lanes)]), axis, ahead)
        from_next = lax.ppermute(jnp.concatenate([flat, to_prev.reshape(-1, lanes)]), axis, behind)
        if axis == "row":
            placed = placed.at[:, 1].add(from_prev[size:].reshape(edge_shape))
            placed = placed.at[:, box_side].add(from_next[size:].reshape(edge_shape))
        else:
            placed = placed.at[:, 1 : box_side + 1, 1].add(from_prev[size:].reshape(edge_shape))
            placed = placed.at[:, 1 : box_side + 1, box_side].add(
                from_next[size:].reshape(edge_shape)
            )
        cells = jnp.concatenate(
            [from_prev[:size].reshape(cells.shape), cells, from_next[:size].reshape(cells.shape)],
            axis=dim,
        )
    return cells.astype(jnp.bfloat16), placed[:, 1 : box_side + 1, 1 : box_side + 1]


def step_order(count):
    minor = 16 if count % 16 == 0 else count
    steps = [1 << b for b in range(count.bit_length() - 1)]
    low = [k for k in steps if k < minor]
    high = [k for k in steps if k >= minor]
    return low[::-1] + high[::-1]


def gather_ordered(block, axis):
    count = lax.axis_size(axis)
    index = lax.axis_index(axis)
    held = block[None]
    steps = step_order(count)
    for step in steps:
        other = lax.ppermute(held, axis, [(i, i ^ step) for i in range(count)])
        lower = (index & step) == 0
        held = jnp.where(
            lower, jnp.concatenate([held, other], 0), jnp.concatenate([other, held], 0)
        )
    bits = len(steps)
    exps = [step.bit_length() - 1 for step in steps]
    perm = [bits - 1 - exps.index(e) for e in range(bits - 1, -1, -1)]
    held = held.reshape((2,) * bits + held.shape[1:])
    held = jnp.transpose(held, perm + list(range(bits, held.ndim)))
    return held.reshape((count,) + block.shape)


def scatter_sum(parts, axis):
    count = lax.axis_size(axis)
    index = lax.axis_index(axis)
    bits = count.bit_length() - 1
    held = parts.reshape((2,) * bits + parts.shape[1:])
    remaining = list(range(bits - 1, -1, -1))
    for exp in range(bits - 1, -1, -1):
        step = 1 << exp
        at = remaining.index(exp)
        upper = (index & step) != 0
        lo = lax.index_in_dim(held, 0, at, keepdims=False)
        hi = lax.index_in_dim(held, 1, at, keepdims=False)
        send = jnp.where(upper, lo, hi)
        keep = jnp.where(upper, hi, lo)
        held = keep + lax.ppermute(send, axis, [(i, i ^ step) for i in range(count)])
        remaining.pop(at)
    return held


def coarse_exchange(top_b, coarse_tab):
    row_count = lax.axis_size("row")
    col_count = lax.axis_size("col")
    row_idx = lax.axis_index("row")
    col_idx = lax.axis_index("col")
    sources = gather_ordered(top_b, "row").astype(jnp.float32)
    zero = jnp.zeros((), jnp.int32)
    fwd_tab = coarse_tab[0]
    fwd = lax.dynamic_slice(
        fwd_tab,
        (zero, row_idx, col_count - 1 - col_idx, zero),
        (2, row_count, col_count, fwd_tab.shape[-1]),
    )
    fwd = jnp.flip(fwd, 1)
    adj = lax.dynamic_slice(
        fwd_tab,
        (zero, row_count - 1 - row_idx, col_idx, zero),
        (2, row_count, col_count, fwd_tab.shape[-1]),
    )
    adj = jnp.flip(adj, 2)
    adj = jnp.stack([adj[0], -adj[1]])
    coeff = jnp.stack([fwd, adj]).astype(jnp.float32)
    src_rows = jnp.arange(row_count)
    dst_cols = jnp.arange(col_count)
    distant = (jnp.abs(row_idx - src_rows)[:, None] > 1) | (jnp.abs(dst_cols - col_idx)[None, :] > 1)
    weight = distant.astype(jnp.float32)[None, :, :, None]
    coef_re = coeff[:, 0] * weight
    coef_im = coeff[:, 1] * weight
    val_re = jnp.moveaxis(sources[:, :, 0], 0, 1)[:, :, None]
    val_im = jnp.moveaxis(sources[:, :, 1], 0, 1)[:, :, None]
    c_re = coef_re[:, :, :, None]
    c_im = coef_im[:, :, :, None]
    got_re = (c_re * val_re - c_im * val_im).sum(1)
    got_im = (c_re * val_im + c_im * val_re).sum(1)
    parts = jnp.moveaxis(jnp.stack([got_re, got_im], 1), 2, 0)
    return scatter_sum(parts, "col")


def leaf_incoming(window, leaf_tab, box_side):
    span = 3 * box_side
    reach = 2 * box_side - 1
    width = 2 * reach + 1
    streams, _, _, _, rhs, dirs = window.shape
    targets = jnp.arange(box_side * box_side)
    cells = jnp.arange(span * span)
    d_row = (cells // span)[None, :] - (targets // box_side)[:, None] + box_side - 1
    d_col = (cells % span)[None, :] - (targets % box_side)[:, None] + box_side - 1
    far_off = (jnp.abs(d_row - reach) > 1) | (jnp.abs(d_col - reach) > 1)
    code = jnp.where(far_off, d_row * width + d_col, -1)
    pick = (code[:, :, None] == jnp.arange(width * width)).astype(jnp.float32)
    flat_tab = leaf_tab.reshape(streams, 2, width * width, dirs)
    coef = jnp.einsum("tnp,sxpq->tnsxq", pick, flat_tab, precision=HIGH)
    win = jnp.moveaxis(window, (2, 3), (0, 1)).reshape(span * span, streams, 2, rhs, dirs)
    c_re = coef[:, :, :, 0, None, :]
    c_im = coef[:, :, :, 1, None, :]
    w_re = win[None, :, :, 0]
    w_im = win[None, :, :, 1]
    in_re = (c_re * w_re - c_im * w_im).sum(1)
    in_im = (c_re * w_im + c_im * w_re).sum(1)
    leaf_in = jnp.stack([in_re, in_im], 2).reshape(box_side, box_side, streams, 2, rhs, dirs)
    return jnp.moveaxis(leaf_in, (0, 1), (2, 3))


def radiate(vectors, rad_tab):
    out_re = product("srcmp,sqp->srcmq", vectors[:, 0], rad_tab[:, 0]) - product(
        "srcmp,sqp->srcmq", vectors[:, 1], rad_tab[:, 1]
    )
    out_im = product("srcmp,sqp->srcmq", vectors[:, 0], rad_tab[:, 1]) + product(
        "srcmp,sqp->srcmq", vectors[:, 1], rad_tab[:, 0]
    )
    return jnp.stack([out_re, out_im], 1)


def far_field(own, vectors, rad_tab, rcv_tab, leaf_tab, coarse_tab, interp, phase):
    box_side = own.shape[2]
    leaf_out = radiate(own, rad_tab)
    window = radiate(vectors, rad_tab)
    leaf_in = leaf_incoming(window, leaf_tab, box_side)
    interpolated = jnp.einsum("kq,sxrcmq->sxrcmk", interp, leaf_out, precision=HIGH)
    angles = phase.reshape(box_side, box_side, -1)
    cos_ph = jnp.cos(angles)[:, :, None, :]
    sin_ph = jnp.sin(angles)[:, :, None, :]
    top_re = (cos_ph * interpolated[:, 0] - sin_ph * interpolated[:, 1]).sum((1, 2))
    top_im = (cos_ph * interpolated[:, 1] + sin_ph * interpolated[:, 0]).sum((1, 2))
    top_b = jnp.stack([top_re, top_im], 1).astype(jnp.bfloat16)
    coarse_in = coarse_exchange(top_b, coarse_tab)
    in_re = coarse_in[:, 0][:, None, None]
    in_im = coarse_in[:, 1][:, None, None]
    back_re = cos_ph * in_re + sin_ph * in_im
    back_im = cos_ph * in_im - sin_ph * in_re
    spread = jnp.einsum(
        "kq,sxrcmk->sxrcmq", interp, jnp.stack([back_re, back_im], 1), precision=HIGH
    )
    incoming = (leaf_in + spread).astype(jnp.bfloat16)
    res_re = product("srcmq,spq->srcmp", incoming[:, 0], rcv_tab[:, 0]) - product(
        "srcmq,spq->srcmp", incoming[:, 1], rcv_tab[:, 1]
    )
    res_im = product("srcmq,spq->srcmp", incoming[:, 0], rcv_tab[:, 1]) + product(
        "srcmq,spq->srcmp", incoming[:, 1], rcv_tab[:, 0]
    )
    return jnp.stack([res_re, res_im], 1)


def per_device_body(
    current,
    probe,
    near_list,
    near_blocks,
    radiation,
    reception,
    interp,
    phase,
    leaf_table,
    coarse_table,
):
    box_side = current.shape[1]
    placed = near_adjoint_local(probe, near_list, near_blocks)
    vectors, near_adj = exchange_halo(jnp.stack([current, probe]), placed)
    padded = vectors[0][:, box_side - 1 : 2 * box_side + 1, box_side - 1 : 2 * box_side + 1]
    near_fwd = near_forward(padded, near_list, near_blocks)
    fwd_set = (radiation, reception, leaf_table, coarse_table)
    adj_set = (
        jnp.stack([reception[0].T, -reception[1].T]),
        jnp.stack([radiation[0].T, -radiation[1].T]),
        conj_flip(leaf_table, (1, 2)),
        None,
    )
    far_both = far_field(
        jnp.stack([current, probe]),
        vectors,
        jnp.stack([fwd_set[0], adj_set[0]]),
        jnp.stack([fwd_set[1], adj_set[1]]),
        jnp.stack([fwd_set[2], adj_set[2]]),
        coarse_table[None],
        interp,
        phase,
    )
    far_fwd = far_both[0]
    far_adj = far_both[1]
    return (near_fwd + far_fwd, near_adj + far_adj)


def solution(mesh):
    placed = (
        P(None, "row", "col", None, None),
        P(None, "row", "col", None, None),
        P("row", "col", None),
        P(None, "row", "col", None, None, None),
        P(),
        P(),
        P(),
        P(),
        P(),
        P(),
    )
    return jax.shard_map(
        per_device_body,
        mesh=mesh,
        in_specs=placed,
        out_specs=(P(None, "row", "col", None, None), P(None, "row", "col", None, None)),
        check_vma=False,
    )
```
